512 devices in a mesh: seq: 32 (over x, y), head: 8 (over z_hi, core), var: 2 (over z_lo).
Axes of the slice: x: 4, y: 8, z: 8 (z_hi: 4, z_lo: 2; z = z_hi * 2 + z_lo), core: 2. Of those that a mesh axis runs over, the one named last changes fastest.
Arguments:
- inner: bfloat16 [2048, 4096], P('seq', 'head'), may hold values from -4.5 to 4.5
- residual_in: bfloat16 [2048, 4096], P('seq', 'head'), may hold values from -6 to 6
- erase: int32 [2, 2048], P('var', 'seq'), parts along dimension 0, may hold values from 0 to 1, as said below
- conv_weight: float32 [4, 4096], P(None, 'head'), may hold values from -3 to 3
- qkv_weight: bfloat16 [8, 512, 1536], P('head'), may hold values from -0.25 to 0.25
- gate_weight: bfloat16 [8, 2, 512], P('head'), may hold values from -0.4075734 to 0.4075734, as said below
- gate_bias: float32 [8, 2], P('head'), as said below
- norm_gain: float32 [4096], P('head'), may hold values from 0.5 to 1.5
- down_weight: bfloat16 [4096, 4096], P('head', 'seq'), may hold values from -0.09375 to 0.09375
Outputs:
- mixed: bfloat16 [2, 2048, 4096], P('var', 'seq', 'head'), parts along dimension 0
The draws below stay inside these ranges and needn't reach their ends.
There are 2 independent parts, one for each index of `var`. The reference program is written for one: setup_inputs(seed, part) draws one part's arguments, and reference() takes and returns one part's arrays. A program takes and returns all parts, laid end to end along the dimension named above; an argument that names none is the same for every part. Nothing has to cross between parts.
Inputs may be any that keep to these rules, and one draw needn't show every extreme that they name: `erase`: each variant erases a few runs of consecutive tokens. `gate_weight`: row 0 of each head holds the input gate projection and row 1 the forget gate projection. `gate_bias`: column 0 is the input gate bias and column 1 the forget gate bias of each head.
All inputs are finite; a program needn't handle non-finite values.
Results may differ from the reference program's by a relative error of at most 0.014.
Values may be sent and summed in bfloat16 or wider, within the bound.
No kernel may reach another device: no remote copies, remote signals or barrier semaphores. Data moves between devices by JAX's collectives and lax.ppermute only.
A program may use at most 128 MiB of HBM per device.

```python
import jax
import jax.numpy as jnp
from jax import lax

D = 4096
DH = 512
CONV = 4
VARS = 1
TOK_DEV = 64
HEADS = 8
INNER = 4096
TOKENS = 2048
N_SEQ = 32


def draw_inner(key, part):
    base_key = jax.random.fold_in(key, 31)
    entries = jnp.clip(jax.random.normal(base_key, (TOKENS, INNER)), -4.5, 4.5)
    return entries.astype(jnp.float32).astype(jnp.bfloat16)


def draw_gate_weight(key, part):
    base_key = jax.random.fold_in(key, 37)
    spread = max(DH // 9, 1) ** (-0.5)
    entries = jnp.clip(jax.random.normal(base_key, (HEADS, 2, DH)), -3.0, 3.0)
    row_scale = jnp.array([0.02, 1.0], jnp.float32)[None, :, None]
    return (entries.astype(jnp.float32) * spread * row_scale).astype(jnp.bfloat16)


def draw_erase(key, part):
    first_key, second_key = jax.random.split(jax.random.fold_in(key, 11), 2)
    span_starts = jax.random.randint(first_key, (VARS, 6), 0, TOKENS)
    span_lengths = jax.random.randint(second_key, (VARS, 6), 1, max(2, TOKENS // 16))
    position = jnp.arange(TOKENS)[None, :, None]
    covered = (position >= span_starts[:, None, :]) & (position < span_starts[:, None, :] + span_lengths[:, None, :])
    return jnp.any(covered, axis=2).astype(jnp.int32)


def draw_gate_bias(key, part):
    order_key, slow_key, fast_key, input_key = jax.random.split(jax.random.fold_in(key, 23), 4)
    order = jax.random.permutation(order_key, HEADS)
    slow_heads = order < max(HEADS // 2, 1)
    slow_bias = jnp.log(TOKENS * 1.0) + jax.random.uniform(slow_key, (HEADS,), minval=0.3, maxval=0.8)
    fast_bias = jax.random.uniform(fast_key, (HEADS,), minval=3.2, maxval=4.2)
    forget_bias = jnp.where(slow_heads, slow_bias, fast_bias)
    input_bias = jax.random.uniform(input_key, (HEADS,), minval=-1.0, maxval=1.0)
    return jnp.stack([input_bias, forget_bias], axis=1).astype(jnp.float32)


def steps_of(own_key, extent, shards, smallest, top_value):
    gain, own = 1.0, jax.random.fold_in(own_key, 6)
    for dim, parts in shards:
        draws = jnp.exp(jax.random.uniform(jax.random.fold_in(own, dim), (parts,), jnp.float32, smallest / len(shards), top_value / len(shards)))
        gain = gain * jnp.repeat(draws, extent[dim] // parts).reshape([-1 if axis == dim else 1 for axis in range(len(extent))])
    return gain


def gaussian(key, dims, scale, bound, pieces=(), kind=jnp.bfloat16):
    loudness = steps_of(key, dims, pieces, -0.22, 0.18) if pieces else 1.0
    values = jax.random.normal(key, dims, jnp.float32) * scale * loudness
    return jnp.minimum(jnp.maximum(values, -bound), bound).astype(kind)


def setup_inputs(seed: int = 0, part: int = 0) -> dict:
    keys = jax.random.split(jax.random.key(seed), 10)
    part_keys = jax.random.split(jax.random.fold_in(keys[9], part), 10)
    inner = draw_inner(jax.random.fold_in(keys[9], 71), part)
    residual_in = gaussian(keys[1], (TOKENS, D), 1.0, 6.0, ((0, 32), (1, 8)))
    erase = draw_erase(jax.random.fold_in(jax.random.fold_in(keys[9], part), 71), part)
    conv_weight = gaussian(keys[3], (CONV, INNER), 0.5, 3.0, ((1, 8),), jnp.float32)
    qkv_weight = gaussian(keys[4], (HEADS, DH, 3 * DH), DH ** -0.5, 0.25, ((0, 8),))
    gate_weight = draw_gate_weight(jax.random.fold_in(keys[9], 71), part)
    gate_bias = draw_gate_bias(jax.random.fold_in(keys[9], 71), part)
    norm_gain = jnp.clip(1.0 + 0.1 * jax.random.normal(keys[7], (INNER,), jnp.float32), 0.5, 1.5)
    down_weight = gaussian(keys[8], (INNER, D), INNER ** -0.5, 0.09375, ((0, 8), (1, 32)))
    return dict(inner=inner, residual_in=residual_in, erase=erase, conv_weight=conv_weight, qkv_weight=qkv_weight, gate_weight=gate_weight, gate_bias=gate_bias, norm_gain=norm_gain, down_weight=down_weight)


def reference(inner, residual_in, erase, conv_weight, qkv_weight, gate_weight, gate_bias, norm_gain, down_weight):
    kept_mask = (1 - erase).astype(jnp.bfloat16)
    erased = inner[None, :, :] * kept_mask[:, :, None]
    padded = jnp.pad(erased, ((0, 0), (CONV - 1, 0), (0, 0)))
    conv_taps = conv_weight.astype(jnp.float32)
    proj_all = qkv_weight.astype(jnp.float32)
    gate_all = gate_weight.astype(jnp.float32)
    gain_heads = norm_gain.astype(jnp.float32).reshape(HEADS, DH)
    causal = jnp.arange(TOK_DEV)[:, None] >= jnp.arange(TOK_DEV)[None, :]

    def block(memory, block_index):
        row_start = (block_index * TOK_DEV).astype(jnp.int32)
        window = lax.dynamic_slice_in_dim(padded, row_start, TOK_DEV + CONV - 1, 1).astype(jnp.float32)
        convolved = jnp.zeros((VARS, TOK_DEV, INNER), jnp.float32)
        for offset in range(CONV):
            convolved = convolved + conv_taps[offset] * window[:, CONV - 1 - offset:CONV - 1 - offset + TOK_DEV]
        activated = jax.nn.silu(convolved).astype(jnp.bfloat16).astype(jnp.float32).reshape(VARS, TOK_DEV, HEADS, DH)
        own_rows = window[:, CONV - 1:].reshape(VARS, TOK_DEV, HEADS, DH)
        query_key = jnp.einsum('vthd,hde->vthe', activated, proj_all[:, :, :2 * DH])
        queries = query_key[..., :DH].astype(jnp.bfloat16).astype(jnp.float32)
        key_rows = (query_key[..., DH:] * DH ** (-0.5)).astype(jnp.bfloat16).astype(jnp.float32)
        values = jnp.einsum('vthd,hde->vthe', own_rows, proj_all[:, :, 2 * DH:]).astype(jnp.bfloat16).astype(jnp.float32)
        gate_pre = jnp.einsum('vthd,hgd->vthg', activated, gate_all) + gate_bias.astype(jnp.float32)
        input_log = 15.0 * jnp.tanh(gate_pre[..., 0] / 15.0)
        forget_log = jax.nn.log_sigmoid(gate_pre[..., 1])
        cumulated = jnp.cumsum(forget_log, axis=1)
        block_decay = cumulated[:, -1]
        scores = jnp.einsum('vthd,vshd->vhts', queries, key_rows)
        cum_heads = jnp.transpose(cumulated, (0, 2, 1))
        in_heads = jnp.transpose(input_log, (0, 2, 1))
        exponent = cum_heads[:, :, :, None] - cum_heads[:, :, None, :] + in_heads[:, :, None, :]
        weights = (scores * jnp.exp(jnp.where(causal, exponent, -jnp.inf))).astype(jnp.bfloat16).astype(jnp.float32)
        intra_part = jnp.einsum('vhts,vshe->vthe', weights, values)
        memory_rounded = lax.optimization_barrier(memory.astype(jnp.bfloat16)).astype(jnp.float32)
        carry_part = jnp.einsum('vthd,vhde->vthe', queries, memory_rounded)
        numerator = jnp.exp(cumulated)[..., None] * carry_part + intra_part
        key_scale = jnp.exp(block_decay[:, None, :] - cumulated + input_log)
        scaled_keys = (key_scale[..., None] * key_rows).astype(jnp.bfloat16).astype(jnp.float32)
        own_memory = jnp.einsum('vshd,vshe->vhde', scaled_keys, values)
        memory = jnp.exp(block_decay)[:, :, None, None] * memory + own_memory
        row_mean = lax.optimization_barrier(jnp.mean(numerator, axis=-1, keepdims=True))
        centred = numerator - row_mean
        row_var = lax.optimization_barrier(jnp.mean(centred * centred, axis=-1, keepdims=True))
        normed = (centred * lax.rsqrt(row_var + 1e-05) * gain_heads).astype(jnp.bfloat16)
        return (memory, normed.reshape(VARS, TOK_DEV, INNER))
    start_memory = jnp.zeros((VARS, HEADS, DH, DH), jnp.float32)
    final_memory, blocks = lax.scan(block, start_memory, jnp.arange(N_SEQ, dtype=jnp.int32))
    normed_all = jnp.transpose(blocks, (1, 0, 2, 3)).reshape(VARS * TOKENS, INNER)

    def add_head(head_index, running_sum):
        head_start = (head_index * DH).astype(jnp.int32)
        head_rows = lax.dynamic_slice_in_dim(normed_all, head_start, DH, 1)
        head_weight = lax.dynamic_slice_in_dim(down_weight, head_start, DH, 0)
        head_part = jnp.dot(head_rows, head_weight, preferred_element_type=jnp.float32).astype(jnp.bfloat16)
        head_part = lax.optimization_barrier(head_part)
        return running_sum + head_part.astype(jnp.float32)
    running_sum = lax.fori_loop(0, HEADS, add_head, jnp.zeros((VARS * TOKENS, D), jnp.float32))
    mixed = residual_in[None, :, :].astype(jnp.float32) + running_sum.reshape(VARS, TOKENS, D)
    return mixed.astype(jnp.bfloat16)
```

```python
import jax
import jax.numpy as jnp
from jax import lax
from jax.sharding import Mesh
from jax.sharding import PartitionSpec as P

CONV = 4
SEQ = ("seq_0", "seq_1")
EXTRA = 16


def from_behind(value, axis, steps):
    count = lax.axis_size(axis)
    initial, last = (max(0, -steps), min(count, count - steps))
    return lax.ppermute(value, axis, [(source, source + steps) for source in range(initial, last)])


def split_up(x, dim, size):
    lengths = x.shape
    blocks = x.reshape(*lengths[:dim], size, lengths[dim] // size, *lengths[dim + 1 :])
    return jnp.moveaxis(blocks, dim, 0)


def sent_and_summed(x, axis, dim):
    blocks = split_up(x, dim, lax.axis_size(axis))
    arrived = lax.all_to_all(blocks, axis, split_axis=0, concat_axis=0, tiled=True)
    return arrived.astype(jnp.float32).sum(axis=0)


def three_parts(x):
    hi = lax.reduce_precision(x, exponent_bits=8, mantissa_bits=7)
    rest = x - hi
    mid = lax.reduce_precision(rest, exponent_bits=8, mantissa_bits=7)
    lo = rest - mid
    return jnp.stack([hi, mid, lo], axis=-1).astype(jnp.bfloat16)


def local_terms(queries, key_rows, values, cumulated, input_log):
    token_count = queries.shape[1]
    causal = jnp.arange(token_count)[:, None] >= jnp.arange(token_count)[None, :]
    scores = jnp.einsum("vtd,vsd->vts", queries, key_rows, preferred_element_type=jnp.float32)
    exponent = cumulated[:, :, None] - cumulated[:, None, :] + input_log[:, None, :]
    weights = (scores * jnp.exp(jnp.where(causal, exponent, -jnp.inf))).astype(jnp.bfloat16)
    return jnp.einsum("vts,vse->vte", weights, values, preferred_element_type=jnp.float32)


def carried_terms(queries, cumulated, gathered, block):
    blocks, rows, head_size = gathered.shape
    token_count = queries.shape[1]
    keys_all = gathered[:, :token_count, :].reshape(blocks * token_count, head_size)
    values_all = gathered[:, token_count : 2 * token_count, :].reshape(blocks * token_count, head_size)
    parts = gathered[:, 2 * token_count, :3].astype(jnp.float32)
    decay = (parts[:, 0] + parts[:, 1]) + parts[:, 2]
    through = jnp.cumsum(decay)
    before_own = jnp.sum(jnp.where(jnp.arange(blocks) < block, decay, 0.0))
    earlier = jnp.arange(blocks) < block
    block_exponent = jnp.where(earlier, before_own - through, -jnp.inf)
    exponent = cumulated[:, :, None, None] + block_exponent[None, None, :, None]
    scale = jnp.exp(jnp.broadcast_to(exponent, (*cumulated.shape, blocks, token_count)))
    scale = scale.reshape(*cumulated.shape, blocks * token_count)
    scores = jnp.einsum("vtd,sd->vts", queries, keys_all, preferred_element_type=jnp.float32)
    weights = scores * scale
    high = weights.astype(jnp.bfloat16)
    low = (weights - high.astype(jnp.float32)).astype(jnp.bfloat16)
    return jnp.einsum("vts,se->vte", high, values_all, preferred_element_type=jnp.float32) + jnp.einsum(
        "vts,se->vte", low, values_all, preferred_element_type=jnp.float32
    )


def body(
    inner,
    residual_in,
    erase,
    conv_weight,
    qkv_weight,
    gate_weight,
    gate_bias,
    norm_gain,
    down_weight,
):
    columns_all = lax.all_gather(down_weight, SEQ, axis=0, tiled=False)
    kept_mask = (1 - erase).astype(jnp.bfloat16)
    erased = inner[None, :, :] * kept_mask[:, :, None]
    row_count = inner.shape[0]
    last_rows = erased[:, row_count - (CONV - 1) :, :]
    prior_rows = from_behind(last_rows, SEQ, 1)
    window = jnp.concatenate([prior_rows, erased], axis=1).astype(jnp.float32)
    convolved = jnp.zeros(erased.shape, jnp.float32)
    for offset in range(CONV):
        convolved = (
            convolved
            + conv_weight[offset] * window[:, CONV - 1 - offset : CONV - 1 - offset + row_count]
        )
    activated = jax.nn.silu(convolved).astype(jnp.bfloat16)
    proj_head = qkv_weight[0]
    head_size = proj_head.shape[0]
    query_key = jnp.einsum(
        "vtd,de->vte", activated, proj_head[:, : 2 * head_size], preferred_element_type=jnp.float32
    )
    queries = query_key[..., :head_size].astype(jnp.bfloat16)
    key_rows = (query_key[..., head_size:] * head_size ** (-0.5)).astype(jnp.bfloat16)
    values = jnp.einsum(
        "vtd,de->vte", erased, proj_head[:, 2 * head_size :], preferred_element_type=jnp.float32
    ).astype(jnp.bfloat16)
    gate_pre = (
        jnp.einsum("vtd,gd->vtg", activated, gate_weight[0], preferred_element_type=jnp.float32)
        + gate_bias[0]
    )
    input_log = 15.0 * jnp.tanh(gate_pre[..., 0] / 15.0)
    forget_log = jax.nn.log_sigmoid(gate_pre[..., 1])
    cumulated = jnp.cumsum(forget_log, axis=1)
    block_decay = cumulated[:, -1]
    key_scale = jnp.exp(block_decay[:, None] - cumulated + input_log)
    scaled_keys = (key_scale[..., None] * key_rows.astype(jnp.float32)).astype(jnp.bfloat16)
    extra = jnp.zeros((EXTRA, head_size), jnp.bfloat16)
    extra = extra.at[0, :3].set(three_parts(block_decay[0]))
    packed = jnp.concatenate([scaled_keys[0], values[0], extra], axis=0)
    gathered = lax.all_gather(packed, SEQ, axis=0, tiled=False)
    block = lax.axis_index(SEQ)
    intra_part = local_terms(queries, key_rows, values, cumulated, input_log)
    numerator = carried_terms(queries, cumulated, gathered, block) + intra_part
    row_mean = jnp.mean(numerator, axis=-1, keepdims=True)
    centred = numerator - row_mean
    row_var = jnp.mean(centred * centred, axis=-1, keepdims=True)
    normed = (centred * lax.rsqrt(row_var + 1e-05) * norm_gain).astype(jnp.bfloat16)
    head_terms = jnp.einsum(
        "vtd,kdc->vtkc", normed, columns_all, preferred_element_type=jnp.float32
    ).astype(jnp.bfloat16)
    head_terms = head_terms.reshape(*normed.shape[:2], -1)
    summed = sent_and_summed(head_terms, "head", 2)
    return (residual_in[None, :, :].astype(jnp.float32) + summed).astype(jnp.bfloat16)


def solution(mesh):
    split = Mesh(
        mesh.devices.reshape(4, 8, mesh.shape["head"], mesh.shape["var"]),
        ("seq_0", "seq_1", "head", "var"),
    )
    placed = (
        P(SEQ, "head"),
        P(SEQ, "head"),
        P("var", SEQ),
        P(None, "head"),
        P("head", None, None),
        P("head", None, None),
        P("head", None),
        P("head"),
        P("head", SEQ),
    )
    return jax.shard_map(
        body, mesh=split, in_specs=placed, out_specs=P("var", SEQ, "head"), check_vma=False
    )
```

```python
import jax
import jax.numpy as jnp
from jax import lax
from jax.sharding import Mesh
from jax.sharding import PartitionSpec as P

CONV = 4
SEQ = ("seq_0", "seq_1")
EXTRA = 16


def from_behind(value, axis, steps):
    count = lax.axis_size(axis)
    initial, last = (max(0, -steps), min(count, count - steps))
    return lax.ppermute(value, axis, [(source, source + steps) for source in range(initial, last)])


def split_up(x, dim, size):
    lengths = x.shape
    blocks = x.reshape(*lengths[:dim], size, lengths[dim] // size, *lengths[dim + 1 :])
    return jnp.moveaxis(blocks, dim, 0)


def sent_and_summed(x, axis, dim):
    blocks = split_up(x, dim, lax.axis_size(axis))
    arrived = lax.all_to_all(blocks, axis, split_axis=0, concat_axis=0, tiled=True)
    return arrived.astype(jnp.float32).sum(axis=0)


def ring_pieces(x, axis, count):
    ahead = [(i, (i + 1) % count) for i in range(count)]
    behind = [(i, (i - 1) % count) for i in range(count)]
    before, after = [], []
    forward = backward = x
    for k in range(1, count // 2 + 1):
        forward = lax.ppermute(forward, axis, ahead)
        before.append(forward)
        if k < count - k:
            backward = lax.ppermute(backward, axis, behind)
            after.append(backward)
    return jnp.stack(before[::-1] + [x] + after)


def three_parts(x):
    hi = lax.reduce_precision(x, exponent_bits=8, mantissa_bits=7)
    rest = x - hi
    mid = lax.reduce_precision(rest, exponent_bits=8, mantissa_bits=7)
    lo = rest - mid
    return jnp.stack([hi, mid, lo], axis=-1).astype(jnp.bfloat16)


def local_terms(queries, key_rows, values, cumulated, input_log):
    token_count = queries.shape[1]
    causal = jnp.arange(token_count)[:, None] >= jnp.arange(token_count)[None, :]
    scores = jnp.einsum("vtd,vsd->vts", queries, key_rows, preferred_element_type=jnp.float32)
    exponent = cumulated[:, :, None] - cumulated[:, None, :] + input_log[:, None, :]
    weights = (scores * jnp.exp(jnp.where(causal, exponent, -jnp.inf))).astype(jnp.bfloat16)
    return jnp.einsum("vts,vse->vte", weights, values, preferred_element_type=jnp.float32)


def carried_terms(queries, cumulated, gathered, block):
    blocks, rows, head_size = gathered.shape
    token_count = queries.shape[1]
    keys_all = gathered[:, :token_count, :].reshape(blocks * token_count, head_size)
    values_all = gathered[:, token_count : 2 * token_count, :].reshape(blocks * token_count, head_size)
    parts = gathered[:, 2 * token_count, :3].astype(jnp.float32)
    decay = (parts[:, 0] + parts[:, 1]) + parts[:, 2]
    through = jnp.cumsum(decay)
    before_own = jnp.sum(jnp.where(jnp.arange(blocks) < block, decay, 0.0))
    earlier = jnp.arange(blocks) < block
    block_exponent = jnp.where(earlier, before_own - through, -jnp.inf)
    exponent = cumulated[:, :, None, None] + block_exponent[None, None, :, None]
    scale = jnp.exp(jnp.broadcast_to(exponent, (*cumulated.shape, blocks, token_count)))
    scale = scale.reshape(*cumulated.shape, blocks * token_count)
    scores = jnp.einsum("vtd,sd->vts", queries, keys_all, preferred_element_type=jnp.float32)
    weights = scores * scale
    high = weights.astype(jnp.bfloat16)
    low = (weights - high.astype(jnp.float32)).astype(jnp.bfloat16)
    return jnp.einsum("vts,se->vte", high, values_all, preferred_element_type=jnp.float32) + jnp.einsum(
        "vts,se->vte", low, values_all, preferred_element_type=jnp.float32
    )


def body(
    inner,
    residual_in,
    erase,
    conv_weight,
    qkv_weight,
    gate_weight,
    gate_bias,
    norm_gain,
    down_weight,
):
    outer, inner_size = (lax.axis_size(SEQ[0]), lax.axis_size(SEQ[1]))
    columns_all = ring_pieces(ring_pieces(down_weight, SEQ[0], outer), SEQ[1], inner_size)
    kept_mask = (1 - erase).astype(jnp.bfloat16)
    erased = inner[None, :, :] * kept_mask[:, :, None]
    row_count = inner.shape[0]
    last_rows = erased[:, row_count - (CONV - 1) :, :]
    prior_rows = from_behind(last_rows, SEQ, 1)
    window = jnp.concatenate([prior_rows, erased], axis=1).astype(jnp.float32)
    convolved = jnp.zeros(erased.shape, jnp.float32)
    for offset in range(CONV):
        convolved = (
            convolved
            + conv_weight[offset] * window[:, CONV - 1 - offset : CONV - 1 - offset + row_count]
        )
    activated = jax.nn.silu(convolved).astype(jnp.bfloat16)
    proj_head = qkv_weight[0]
    head_size = proj_head.shape[0]
    query_key = jnp.einsum(
        "vtd,de->vte", activated, proj_head[:, : 2 * head_size], preferred_element_type=jnp.float32
    )
    queries = query_key[..., :head_size].astype(jnp.bfloat16)
    key_rows = (query_key[..., head_size:] * head_size ** (-0.5)).astype(jnp.bfloat16)
    values = jnp.einsum(
        "vtd,de->vte", erased, proj_head[:, 2 * head_size :], preferred_element_type=jnp.float32
    ).astype(jnp.bfloat16)
    gate_pre = (
        jnp.einsum("vtd,gd->vtg", activated, gate_weight[0], preferred_element_type=jnp.float32)
        + gate_bias[0]
    )
    input_log = 15.0 * jnp.tanh(gate_pre[..., 0] / 15.0)
    forget_log = jax.nn.log_sigmoid(gate_pre[..., 1])
    cumulated = jnp.cumsum(forget_log, axis=1)
    block_decay = cumulated[:, -1]
    key_scale = jnp.exp(block_decay[:, None] - cumulated + input_log)
    scaled_keys = (key_scale[..., None] * key_rows.astype(jnp.float32)).astype(jnp.bfloat16)
    extra = jnp.zeros((EXTRA, head_size), jnp.bfloat16)
    extra = extra.at[0, :3].set(three_parts(block_decay[0]))
    packed = jnp.concatenate([scaled_keys[0], values[0], extra], axis=0)
    gathered = lax.all_gather(packed, SEQ, axis=0, tiled=False)
    block = lax.axis_index(SEQ)
    intra_part = local_terms(queries, key_rows, values, cumulated, input_log)
    numerator = carried_terms(queries, cumulated, gathered, block) + intra_part
    row_mean = jnp.mean(numerator, axis=-1, keepdims=True)
    centred = numerator - row_mean
    row_var = jnp.mean(centred * centred, axis=-1, keepdims=True)
    normed = (centred * lax.rsqrt(row_var + 1e-05) * norm_gain).astype(jnp.bfloat16)
    head_terms = jnp.einsum(
        "vtr,edrc->vtedc", normed, columns_all.reshape(inner_size, outer, head_size, -1),
        preferred_element_type=jnp.float32,
    ).astype(jnp.bfloat16)
    head_terms = jnp.roll(head_terms, lax.axis_index(SEQ[1]) - inner_size // 2, axis=2)
    head_terms = jnp.roll(head_terms, lax.axis_index(SEQ[0]) - outer // 2, axis=3)
    head_terms = jnp.swapaxes(head_terms, 2, 3).reshape(*normed.shape[:2], -1)
    summed = sent_and_summed(head_terms, "head", 2)
    return (residual_in[None, :, :].astype(jnp.float32) + summed).astype(jnp.bfloat16)


def solution(mesh):
    split = Mesh(
        mesh.devices.reshape(4, 8, mesh.shape["head"], mesh.shape["var"]),
        ("seq_0", "seq_1", "head", "var"),
    )
    placed = (
        P(SEQ, "head"),
        P(SEQ, "head"),
        P("var", SEQ),
        P(None, "head"),
        P("head", None, None),
        P("head", None, None),
        P("head", None),
        P("head"),
        P("head", SEQ),
    )
    return jax.shard_map(
        body, mesh=split, in_specs=placed, out_specs=P("var", SEQ, "head"), check_vma=False
    )
```

```python
import jax
import jax.numpy as jnp
from jax import lax
from jax.sharding import Mesh
from jax.sharding import PartitionSpec as P

CONV = 4
SEQ = ("seq_0", "seq_1")
EXTRA = 16


def from_behind(value, axis, steps):
    count = lax.axis_size(axis)
    initial, last = (max(0, -steps), min(count, count - steps))
    return lax.ppermute(value, axis, [(source, source + steps) for source in range(initial, last)])


def split_up(x, dim, size):
    lengths = x.shape
    blocks = x.reshape(*lengths[:dim], size, lengths[dim] // size, *lengths[dim + 1 :])
    return jnp.moveaxis(blocks, dim, 0)


def sent_and_summed(x, axis, dim):
    blocks = split_up(x, dim, lax.axis_size(axis))
    arrived = lax.all_to_all(blocks, axis, split_axis=0, concat_axis=0, tiled=True)
    return arrived.astype(jnp.float32).sum(axis=0)


def ring_pieces(x, axis, count):
    ahead = [(i, (i + 1) % count) for i in range(count)]
    behind = [(i, (i - 1) % count) for i in range(count)]
    before, after = [], []
    forward = backward = x
    for k in range(1, count // 2 + 1):
        forward = lax.ppermute(forward, axis, ahead)
        before.append(forward)
        if k < count - k:
            backward = lax.ppermute(backward, axis, behind)
            after.append(backward)
    return jnp.stack(before[::-1] + [x] + after)


def three_parts(x):
    hi = lax.reduce_precision(x, exponent_bits=8, mantissa_bits=7)
    rest = x - hi
    mid = lax.reduce_precision(rest, exponent_bits=8, mantissa_bits=7)
    lo = rest - mid
    return jnp.stack([hi, mid, lo], axis=-1).astype(jnp.bfloat16)


def local_terms(queries, key_rows, values, cumulated, input_log):
    token_count = queries.shape[1]
    causal = jnp.arange(token_count)[:, None] >= jnp.arange(token_count)[None, :]
    scores = jnp.einsum("vtd,vsd->vts", queries, key_rows, preferred_element_type=jnp.float32)
    exponent = cumulated[:, :, None] - cumulated[:, None, :] + input_log[:, None, :]
    weights = (scores * jnp.exp(jnp.where(causal, exponent, -jnp.inf))).astype(jnp.bfloat16)
    return jnp.einsum("vts,vse->vte", weights, values, preferred_element_type=jnp.float32)


def exact_pair(x):
    high = x.astype(jnp.bfloat16)
    return high, (x - high.astype(jnp.float32)).astype(jnp.bfloat16)


def two_pass(spec, left, right):
    high, low = exact_pair(left)
    return jnp.einsum(spec, high, right, preferred_element_type=jnp.float32) + jnp.einsum(
        spec, low, right, preferred_element_type=jnp.float32
    )


def block_decays(gathered, token_count):
    parts = gathered[:, 2 * token_count, :3].astype(jnp.float32)
    return (parts[:, 0] + parts[:, 1]) + parts[:, 2]


def carried_terms(queries, cumulated, gathered, block):
    blocks, rows, head_size = gathered.shape
    token_count = queries.shape[1]
    keys_all = gathered[:, :token_count, :].reshape(blocks * token_count, head_size)
    values_all = gathered[:, token_count : 2 * token_count, :].reshape(blocks * token_count, head_size)
    decay = block_decays(gathered, token_count)
    through = jnp.cumsum(decay)
    earlier = jnp.arange(blocks) < block
    before_own = jnp.sum(jnp.where(earlier, decay, 0.0))
    block_exponent = jnp.where(earlier, before_own - through, -jnp.inf)
    exponent = cumulated[:, :, None, None] + block_exponent[None, None, :, None]
    scale = jnp.exp(jnp.broadcast_to(exponent, (*cumulated.shape, blocks, token_count)))
    scale = scale.reshape(*cumulated.shape, blocks * token_count)
    scores = jnp.einsum("vtd,sd->vts", queries, keys_all, preferred_element_type=jnp.float32)
    return two_pass("vts,se->vte", scores * scale, values_all), before_own


def group_rows(gathered, token_count, rows_at, row_count):
    decay = block_decays(gathered, token_count)
    tail = jnp.sum(decay) - jnp.cumsum(decay)
    keys = lax.dynamic_slice_in_dim(gathered[:, :token_count, :], rows_at, row_count, 2)
    values = gathered[:, token_count : 2 * token_count, :]
    scaled = keys.astype(jnp.float32) * jnp.exp(tail)[:, None, None]
    return two_pass("jtr,jte->re", scaled, values), jnp.sum(decay)


def body(
    inner,
    residual_in,
    erase,
    conv_weight,
    qkv_weight,
    gate_weight,
    gate_bias,
    norm_gain,
    down_weight,
):
    outer, inner_size = (lax.axis_size(SEQ[0]), lax.axis_size(SEQ[1]))
    columns_all = ring_pieces(ring_pieces(down_weight, SEQ[0], outer), SEQ[1], inner_size)
    kept_mask = (1 - erase).astype(jnp.bfloat16)
    erased = inner[None, :, :] * kept_mask[:, :, None]
    row_count = inner.shape[0]
    last_rows = erased[:, row_count - (CONV - 1) :, :]
    prior_rows = from_behind(last_rows, SEQ, 1)
    window = jnp.concatenate([prior_rows, erased], axis=1).astype(jnp.float32)
    convolved = jnp.zeros(erased.shape, jnp.float32)
    for offset in range(CONV):
        convolved = (
            convolved
            + conv_weight[offset] * window[:, CONV - 1 - offset : CONV - 1 - offset + row_count]
        )
    activated = jax.nn.silu(convolved).astype(jnp.bfloat16)
    proj_head = qkv_weight[0]
    head_size = proj_head.shape[0]
    query_key = jnp.einsum(
        "vtd,de->vte", activated, proj_head[:, : 2 * head_size], preferred_element_type=jnp.float32
    )
    queries = query_key[..., :head_size].astype(jnp.bfloat16)
    key_rows = (query_key[..., head_size:] * head_size ** (-0.5)).astype(jnp.bfloat16)
    values = jnp.einsum(
        "vtd,de->vte", erased, proj_head[:, 2 * head_size :], preferred_element_type=jnp.float32
    ).astype(jnp.bfloat16)
    gate_pre = (
        jnp.einsum("vtd,gd->vtg", activated, gate_weight[0], preferred_element_type=jnp.float32)
        + gate_bias[0]
    )
    input_log = 15.0 * jnp.tanh(gate_pre[..., 0] / 15.0)
    forget_log = jax.nn.log_sigmoid(gate_pre[..., 1])
    cumulated = jnp.cumsum(forget_log, axis=1)
    block_decay = cumulated[:, -1]
    key_scale = jnp.exp(block_decay[:, None] - cumulated + input_log)
    scaled_keys = (key_scale[..., None] * key_rows.astype(jnp.float32)).astype(jnp.bfloat16)
    extra = jnp.zeros((EXTRA, head_size), jnp.bfloat16)
    extra = extra.at[0, :3].set(three_parts(block_decay[0]))
    packed = jnp.concatenate([scaled_keys[0], values[0], extra], axis=0)
    gathered = lax.all_gather(packed, SEQ[1], axis=0, tiled=False)
    place, group = (lax.axis_index(SEQ[1]), lax.axis_index(SEQ[0]))
    slice_rows = head_size // inner_size
    within, before_own = carried_terms(queries, cumulated, gathered, place)
    leaving, group_decay = group_rows(gathered, row_count, place * slice_rows, slice_rows)
    group_extra = jnp.zeros((8, head_size), jnp.float32).at[0, 0].set(group_decay)
    across = lax.all_gather(jnp.concatenate([leaving, group_extra], axis=0), SEQ[0], axis=0, tiled=False)
    decays = across[:, slice_rows, 0]
    earlier = jnp.arange(outer) < group
    before_group = jnp.sum(jnp.where(earlier, decays, 0.0))
    factor = jnp.where(earlier, jnp.exp(jnp.where(earlier, before_group - jnp.cumsum(decays), 0.0)), 0.0)
    entering_rows = jnp.sum(factor[:, None, None] * across[:, :slice_rows, :], axis=0)
    entering = lax.all_gather(entering_rows, SEQ[1], axis=0, tiled=True)
    carried = two_pass("vde,vtd->vte", entering[None], queries)
    carried = jnp.exp(cumulated + before_own)[..., None] * carried
    intra_part = local_terms(queries, key_rows, values, cumulated, input_log)
    numerator = (carried + within) + intra_part
    row_mean = jnp.mean(numerator, axis=-1, keepdims=True)
    centred = numerator - row_mean
    row_var = jnp.mean(centred * centred, axis=-1, keepdims=True)
    normed = (centred * lax.rsqrt(row_var + 1e-05) * norm_gain).astype(jnp.bfloat16)
    head_terms = jnp.einsum(
        "vtr,edrc->vtedc", normed, columns_all.reshape(inner_size, outer, head_size, -1),
        preferred_element_type=jnp.float32,
    ).astype(jnp.bfloat16)
    head_terms = jnp.roll(head_terms, lax.axis_index(SEQ[1]) - inner_size // 2, axis=2)
    head_terms = jnp.roll(head_terms, lax.axis_index(SEQ[0]) - outer // 2, axis=3)
    head_terms = jnp.swapaxes(head_terms, 2, 3).reshape(*normed.shape[:2], -1)
    summed = sent_and_summed(head_terms, "head", 2)
    return (residual_in[None, :, :].astype(jnp.float32) + summed).astype(jnp.bfloat16)


def solution(mesh):
    split = Mesh(
        mesh.devices.reshape(4, 8, mesh.shape["head"], mesh.shape["var"]),
        ("seq_0", "seq_1", "head", "var"),
    )
    placed = (
        P(SEQ, "head"),
        P(SEQ, "head"),
        P("var", SEQ),
        P(None, "head"),
        P("head", None, None),
        P("head", None, None),
        P("head", None),
        P("head"),
        P("head", SEQ),
    )
    return jax.shard_map(
        body, mesh=split, in_specs=placed, out_specs=P("var", SEQ, "head"), check_vma=False
    )
```

```python
import jax
import jax.numpy as jnp
from jax import lax
from jax.sharding import Mesh
from jax.sharding import PartitionSpec as P

CONV = 4
SEQ = ("seq_0", "seq_1")
EXTRA = 16


def from_behind(value, axis, steps):
    count = lax.axis_size(axis)
    initial, last = (max(0, -steps), min(count, count - steps))
    return lax.ppermute(value, axis, [(source, source + steps) for source in range(initial, last)])


def split_up(x, dim, size):
    lengths = x.shape
    blocks = x.reshape(*lengths[:dim], size, lengths[dim] // size, *lengths[dim + 1 :])
    return jnp.moveaxis(blocks, dim, 0)


def sent_and_summed(x, axis, dim):
    blocks = split_up(x, dim, lax.axis_size(axis))
    arrived = lax.all_to_all(blocks, axis, split_axis=0, concat_axis=0, tiled=True)
    return arrived.astype(jnp.float32).sum(axis=0)


def exchanged_and_summed(x, axis, dim):
    count = lax.axis_size(axis)
    blocks = split_up(x, dim, count)
    turned = jnp.roll(blocks, -lax.axis_index(axis), axis=0)
    total = turned[0].astype(jnp.float32)
    for k in range(1, count):
        moved = lax.ppermute(turned[k], axis, [(i, (i + k) % count) for i in range(count)])
        total = total + moved.astype(jnp.float32)
    return total


def ring_pieces(x, axis, count):
    ahead = [(i, (i + 1) % count) for i in range(count)]
    behind = [(i, (i - 1) % count) for i in range(count)]
    before, after = [], []
    forward = backward = x
    for k in range(1, count // 2 + 1):
        forward = lax.ppermute(forward, axis, ahead)
        before.append(forward)
        if k < count - k:
            backward = lax.ppermute(backward, axis, behind)
            after.append(backward)
    return jnp.stack(before[::-1] + [x] + after)


def three_parts(x):
    hi = lax.reduce_precision(x, exponent_bits=8, mantissa_bits=7)
    rest = x - hi
    mid = lax.reduce_precision(rest, exponent_bits=8, mantissa_bits=7)
    lo = rest - mid
    return jnp.stack([hi, mid, lo], axis=-1).astype(jnp.bfloat16)


def local_terms(queries, key_rows, values, cumulated, input_log):
    token_count = queries.shape[1]
    causal = jnp.arange(token_count)[:, None] >= jnp.arange(token_count)[None, :]
    scores = jnp.einsum("vtd,vsd->vts", queries, key_rows, preferred_element_type=jnp.float32)
    exponent = cumulated[:, :, None] - cumulated[:, None, :] + input_log[:, None, :]
    weights = (scores * jnp.exp(jnp.where(causal, exponent, -jnp.inf))).astype(jnp.bfloat16)
    return jnp.einsum("vts,vse->vte", weights, values, preferred_element_type=jnp.float32)


def carried_terms(queries, cumulated, gathered, block):
    blocks, rows, head_size = gathered.shape
    token_count = queries.shape[1]
    keys_all = gathered[:, :token_count, :].reshape(blocks * token_count, head_size)
    values_all = gathered[:, token_count : 2 * token_count, :].reshape(blocks * token_count, head_size)
    parts = gathered[:, 2 * token_count, :3].astype(jnp.float32)
    decay = (parts[:, 0] + parts[:, 1]) + parts[:, 2]
    through = jnp.cumsum(decay)
    before_own = jnp.sum(jnp.where(jnp.arange(blocks) < block, decay, 0.0))
    earlier = jnp.arange(blocks) < block
    block_exponent = jnp.where(earlier, before_own - through, -jnp.inf)
    exponent = cumulated[:, :, None, None] + block_exponent[None, None, :, None]
    scale = jnp.exp(jnp.broadcast_to(exponent, (*cumulated.shape, blocks, token_count)))
    scale = scale.reshape(*cumulated.shape, blocks * token_count)
    scores = jnp.einsum("vtd,sd->vts", queries, keys_all, preferred_element_type=jnp.float32)
    weights = scores * scale
    high = weights.astype(jnp.bfloat16)
    low = (weights - high.astype(jnp.float32)).astype(jnp.bfloat16)
    return jnp.einsum("vts,se->vte", high, values_all, preferred_element_type=jnp.float32) + jnp.einsum(
        "vts,se->vte", low, values_all, preferred_element_type=jnp.float32
    )


def body(
    inner,
    residual_in,
    erase,
    conv_weight,
    qkv_weight,
    gate_weight,
    gate_bias,
    norm_gain,
    down_weight,
):
    outer, inner_size = (lax.axis_size(SEQ[0]), lax.axis_size(SEQ[1]))
    columns_all = ring_pieces(ring_pieces(down_weight, SEQ[0], outer), SEQ[1], inner_size)
    kept_mask = (1 - erase).astype(jnp.bfloat16)
    erased = inner[None, :, :] * kept_mask[:, :, None]
    row_count = inner.shape[0]
    last_rows = erased[:, row_count - (CONV - 1) :, :]
    prior_rows = from_behind(last_rows, SEQ, 1)
    window = jnp.concatenate([prior_rows, erased], axis=1).astype(jnp.float32)
    convolved = jnp.zeros(erased.shape, jnp.float32)
    for offset in range(CONV):
        convolved = (
            convolved
            + conv_weight[offset] * window[:, CONV - 1 - offset : CONV - 1 - offset + row_count]
        )
    activated = jax.nn.silu(convolved).astype(jnp.bfloat16)
    proj_head = qkv_weight[0]
    head_size = proj_head.shape[0]
    query_key = jnp.einsum(
        "vtd,de->vte", activated, proj_head[:, : 2 * head_size], preferred_element_type=jnp.float32
    )
    queries = query_key[..., :head_size].astype(jnp.bfloat16)
    key_rows = (query_key[..., head_size:] * head_size ** (-0.5)).astype(jnp.bfloat16)
    values = jnp.einsum(
        "vtd,de->vte", erased, proj_head[:, 2 * head_size :], preferred_element_type=jnp.float32
    ).astype(jnp.bfloat16)
    gate_pre = (
        jnp.einsum("vtd,gd->vtg", activated, gate_weight[0], preferred_element_type=jnp.float32)
        + gate_bias[0]
    )
    input_log = 15.0 * jnp.tanh(gate_pre[..., 0] / 15.0)
    forget_log = jax.nn.log_sigmoid(gate_pre[..., 1])
    cumulated = jnp.cumsum(forget_log, axis=1)
    block_decay = cumulated[:, -1]
    key_scale = jnp.exp(block_decay[:, None] - cumulated + input_log)
    scaled_keys = (key_scale[..., None] * key_rows.astype(jnp.float32)).astype(jnp.bfloat16)
    extra = jnp.zeros((EXTRA, head_size), jnp.bfloat16)
    extra = extra.at[0, :3].set(three_parts(block_decay[0]))
    packed = jnp.concatenate([scaled_keys[0], values[0], extra], axis=0)
    gathered = lax.all_gather(packed, SEQ, axis=0, tiled=False)
    block = lax.axis_index(SEQ)
    intra_part = local_terms(queries, key_rows, values, cumulated, input_log)
    numerator = carried_terms(queries, cumulated, gathered, block) + intra_part
    row_mean = jnp.mean(numerator, axis=-1, keepdims=True)
    centred = numerator - row_mean
    row_var = jnp.mean(centred * centred, axis=-1, keepdims=True)
    normed = (centred * lax.rsqrt(row_var + 1e-05) * norm_gain).astype(jnp.bfloat16)
    head_terms = jnp.einsum(
        "vtr,edrc->vtedc", normed, columns_all.reshape(inner_size, outer, head_size, -1),
        preferred_element_type=jnp.float32,
    ).astype(jnp.bfloat16)
    head_terms = jnp.roll(head_terms, lax.axis_index(SEQ[1]) - inner_size // 2, axis=2)
    head_terms = jnp.roll(head_terms, lax.axis_index(SEQ[0]) - outer // 2, axis=3)
    head_terms = jnp.swapaxes(head_terms, 2, 3).reshape(*normed.shape[:2], -1)
    summed = exchanged_and_summed(head_terms, "head", 2)
    return (residual_in[None, :, :].astype(jnp.float32) + summed).astype(jnp.bfloat16)


def solution(mesh):
    split = Mesh(
        mesh.devices.reshape(4, 8, mesh.shape["head"], mesh.shape["var"]),
        ("seq_0", "seq_1", "head", "var"),
    )
    placed = (
        P(SEQ, "head"),
        P(SEQ, "head"),
        P("var", SEQ),
        P(None, "head"),
        P("head", None, None),
        P("head", None, None),
        P("head", None),
        P("head"),
        P("head", SEQ),
    )
    return jax.shard_map(
        body, mesh=split, in_specs=placed, out_specs=P("var", SEQ, "head"), check_vma=False
    )
```

```python
import jax
import jax.numpy as jnp
from jax import lax
from jax.sharding import Mesh
from jax.sharding import PartitionSpec as P

CONV = 4
SEQ = ("seq_0", "seq_1")
EXTRA = 16


def from_behind(value, axis, steps):
    count = lax.axis_size(axis)
    initial, last = (max(0, -steps), min(count, count - steps))
    return lax.ppermute(value, axis, [(source, source + steps) for source in range(initial, last)])


def split_up(x, dim, size):
    lengths = x.shape
    blocks = x.reshape(*lengths[:dim], size, lengths[dim] // size, *lengths[dim + 1 :])
    return jnp.moveaxis(blocks, dim, 0)


def sent_and_summed(x, axis, dim):
    blocks = split_up(x, dim, lax.axis_size(axis))
    arrived = lax.all_to_all(blocks, axis, split_axis=0, concat_axis=0, tiled=True)
    return arrived.astype(jnp.float32).sum(axis=0)


def ring_pieces(x, axis, count):
    ahead = [(i, (i + 1) % count) for i in range(count)]
    behind = [(i, (i - 1) % count) for i in range(count)]
    before, after = [], []
    forward = backward = x
    for k in range(1, count // 2 + 1):
        forward = lax.ppermute(forward, axis, ahead)
        before.append(forward)
        if k < count - k:
            backward = lax.ppermute(backward, axis, behind)
            after.append(backward)
    return jnp.stack(before[::-1] + [x] + after)


def three_parts(x):
    hi = lax.reduce_precision(x, exponent_bits=8, mantissa_bits=7)
    rest = x - hi
    mid = lax.reduce_precision(rest, exponent_bits=8, mantissa_bits=7)
    lo = rest - mid
    return jnp.stack([hi, mid, lo], axis=-1).astype(jnp.bfloat16)


def local_terms(queries, key_rows, values, cumulated, input_log):
    token_count = queries.shape[1]
    causal = jnp.arange(token_count)[:, None] >= jnp.arange(token_count)[None, :]
    scores = jnp.einsum("vtd,vsd->vts", queries, key_rows, preferred_element_type=jnp.float32)
    exponent = cumulated[:, :, None] - cumulated[:, None, :] + input_log[:, None, :]
    weights = (scores * jnp.exp(jnp.where(causal, exponent, -jnp.inf))).astype(jnp.bfloat16)
    return jnp.einsum("vts,vse->vte", weights, values, preferred_element_type=jnp.float32)


def carried_terms(queries, cumulated, gathered, block):
    blocks, rows, head_size = gathered.shape
    token_count = queries.shape[1]
    keys_all = gathered[:, :token_count, :].reshape(blocks * token_count, head_size)
    values_all = gathered[:, token_count : 2 * token_count, :].reshape(blocks * token_count, head_size)
    parts = gathered[:, 2 * token_count, :3].astype(jnp.float32)
    decay = (parts[:, 0] + parts[:, 1]) + parts[:, 2]
    through = jnp.cumsum(decay)
    before_own = jnp.sum(jnp.where(jnp.arange(blocks) < block, decay, 0.0))
    earlier = jnp.arange(blocks) < block
    block_exponent = jnp.where(earlier, before_own - through, -jnp.inf)
    exponent = cumulated[:, :, None, None] + block_exponent[None, None, :, None]
    scale = jnp.exp(jnp.broadcast_to(exponent, (*cumulated.shape, blocks, token_count)))
    scale = scale.reshape(*cumulated.shape, blocks * token_count)
    scores = jnp.einsum("vtd,sd->vts", queries, keys_all, preferred_element_type=jnp.float32)
    weights = scores * scale
    high = weights.astype(jnp.bfloat16)
    low = (weights - high.astype(jnp.float32)).astype(jnp.bfloat16)
    return jnp.einsum("vts,se->vte", high, values_all, preferred_element_type=jnp.float32) + jnp.einsum(
        "vts,se->vte", low, values_all, preferred_element_type=jnp.float32
    )


def body(
    inner,
    residual_in,
    erase,
    conv_weight,
    qkv_weight,
    gate_weight,
    gate_bias,
    norm_gain,
    down_weight,
):
    columns_all = lax.all_gather(down_weight, SEQ, axis=0, tiled=False)
    kept_mask = (1 - erase).astype(jnp.bfloat16)
    erased = inner[None, :, :] * kept_mask[:, :, None]
    row_count = inner.shape[0]
    last_rows = erased[:, row_count - (CONV - 1) :, :]
    prior_rows = from_behind(last_rows, SEQ, 1)
    window = jnp.concatenate([prior_rows, erased], axis=1).astype(jnp.float32)
    convolved = jnp.zeros(erased.shape, jnp.float32)
    for offset in range(CONV):
        convolved = (
            convolved
            + conv_weight[offset] * window[:, CONV - 1 - offset : CONV - 1 - offset + row_count]
        )
    activated = jax.nn.silu(convolved).astype(jnp.bfloat16)
    proj_head = qkv_weight[0]
    head_size = proj_head.shape[0]
    query_key = jnp.einsum(
        "vtd,de->vte", activated, proj_head[:, : 2 * head_size], preferred_element_type=jnp.float32
    )
    queries = query_key[..., :head_size].astype(jnp.bfloat16)
    key_rows = (query_key[..., head_size:] * head_size ** (-0.5)).astype(jnp.bfloat16)
    values = jnp.einsum(
        "vtd,de->vte", erased, proj_head[:, 2 * head_size :], preferred_element_type=jnp.float32
    ).astype(jnp.bfloat16)
    gate_pre = (
        jnp.einsum("vtd,gd->vtg", activated, gate_weight[0], preferred_element_type=jnp.float32)
        + gate_bias[0]
    )
    input_log = 15.0 * jnp.tanh(gate_pre[..., 0] / 15.0)
    forget_log = jax.nn.log_sigmoid(gate_pre[..., 1])
    cumulated = jnp.cumsum(forget_log, axis=1)
    block_decay = cumulated[:, -1]
    key_scale = jnp.exp(block_decay[:, None] - cumulated + input_log)
    scaled_keys = (key_scale[..., None] * key_rows.astype(jnp.float32)).astype(jnp.bfloat16)
    extra = jnp.zeros((EXTRA, head_size), jnp.bfloat16)
    extra = extra.at[0, :3].set(three_parts(block_decay[0]))
    packed = jnp.concatenate([scaled_keys[0], values[0], extra], axis=0)
    shards = lax.axis_size(SEQ)
    copies = jnp.broadcast_to(packed[None], (shards, *packed.shape))
    gathered = lax.all_to_all(copies, SEQ, split_axis=0, concat_axis=0, tiled=True)
    block = lax.axis_index(SEQ)
    intra_part = local_terms(queries, key_rows, values, cumulated, input_log)
    numerator = carried_terms(queries, cumulated, gathered, block) + intra_part
    row_mean = jnp.mean(numerator, axis=-1, keepdims=True)
    centred = numerator - row_mean
    row_var = jnp.mean(centred * centred, axis=-1, keepdims=True)
    normed = (centred * lax.rsqrt(row_var + 1e-05) * norm_gain).astype(jnp.bfloat16)
    head_terms = jnp.einsum(
        "vtd,kdc->vtkc", normed, columns_all, preferred_element_type=jnp.float32
    ).astype(jnp.bfloat16)
    head_terms = head_terms.reshape(*normed.shape[:2], -1)
    summed = sent_and_summed(head_terms, "head", 2)
    return (residual_in[None, :, :].astype(jnp.float32) + summed).astype(jnp.bfloat16)


def solution(mesh):
    split = Mesh(
        mesh.devices.reshape(4, 8, mesh.shape["head"], mesh.shape["var"]),
        ("seq_0", "seq_1", "head", "var"),
    )
    placed = (
        P(SEQ, "head"),
        P(SEQ, "head"),
        P("var", SEQ),
        P(None, "head"),
        P("head", None, None),
        P("head", None, None),
        P("head", None),
        P("head"),
        P("head", SEQ),
    )
    return jax.shard_map(
        body, mesh=split, in_specs=placed, out_specs=P("var", SEQ, "head"), check_vma=False
    )
```

```python
import jax
import jax.numpy as jnp
from jax import lax
from jax.sharding import Mesh
from jax.sharding import PartitionSpec as P

CONV = 4
SEQ = ("seq_0", "seq_1")
EXTRA = 8


def from_behind(value, axis, steps):
    count = lax.axis_size(axis)
    initial, last = (max(0, -steps), min(count, count - steps))
    return lax.ppermute(value, axis, [(source, source + steps) for source in range(initial, last)])


def split_up(x, dim, size):
    lengths = x.shape
    blocks = x.reshape(*lengths[:dim], size, lengths[dim] // size, *lengths[dim + 1 :])
    return jnp.moveaxis(blocks, dim, 0)


def sent_and_summed(x, axis, dim):
    blocks = split_up(x, dim, lax.axis_size(axis))
    arrived = lax.all_to_all(blocks, axis, split_axis=0, concat_axis=0, tiled=True)
    return arrived.astype(jnp.float32).sum(axis=0)


def ring_pieces(x, axis, count):
    ahead = [(i, (i + 1) % count) for i in range(count)]
    behind = [(i, (i - 1) % count) for i in range(count)]
    before, after = [], []
    forward = backward = x
    for k in range(1, count // 2 + 1):
        forward = lax.ppermute(forward, axis, ahead)
        before.append(forward)
        if k < count - k:
            backward = lax.ppermute(backward, axis, behind)
            after.append(backward)
    return jnp.stack(before[::-1] + [x] + after)


def three_parts(x):
    hi = lax.reduce_precision(x, exponent_bits=8, mantissa_bits=7)
    rest = x - hi
    mid = lax.reduce_precision(rest, exponent_bits=8, mantissa_bits=7)
    lo = rest - mid
    return jnp.stack([hi, mid, lo], axis=-1).astype(jnp.bfloat16)


def local_terms(queries, key_rows, values, cumulated, input_log):
    token_count = queries.shape[1]
    causal = jnp.arange(token_count)[:, None] >= jnp.arange(token_count)[None, :]
    scores = jnp.einsum("vtd,vsd->vts", queries, key_rows, preferred_element_type=jnp.float32)
    exponent = cumulated[:, :, None] - cumulated[:, None, :] + input_log[:, None, :]
    weights = (scores * jnp.exp(jnp.where(causal, exponent, -jnp.inf))).astype(jnp.bfloat16)
    return jnp.einsum("vts,vse->vte", weights, values, preferred_element_type=jnp.float32)


def carried_terms(queries, cumulated, gathered, block):
    blocks, rows, _ = gathered.shape
    token_count = queries.shape[1]
    parts = gathered[:, 2 * token_count, :3].astype(jnp.float32)
    decay = (parts[:, 0] + parts[:, 1]) + parts[:, 2]
    through = jnp.cumsum(decay)
    earlier = jnp.arange(blocks) < block
    before_own = jnp.sum(jnp.where(earlier, decay, 0.0))
    block_exponent = jnp.where(earlier, before_own - through, -jnp.inf)
    scale = jnp.exp(cumulated[:, :, None, None] + block_exponent[None, None, :, None])
    scores = jnp.einsum("vtd,brd->vtbr", queries, gathered, preferred_element_type=jnp.float32)
    weights = scores[..., :token_count] * scale
    weights = jnp.pad(weights, ((0, 0), (0, 0), (0, 0), (token_count, rows - 2 * token_count)))
    high = weights.astype(jnp.bfloat16)
    low = (weights - high.astype(jnp.float32)).astype(jnp.bfloat16)
    return jnp.einsum("vtbr,bre->vte", high, gathered, preferred_element_type=jnp.float32) + jnp.einsum(
        "vtbr,bre->vte", low, gathered, preferred_element_type=jnp.float32
    )


def body(
    inner,
    residual_in,
    erase,
    conv_weight,
    qkv_weight,
    gate_weight,
    gate_bias,
    norm_gain,
    down_weight,
):
    outer, inner_size = (lax.axis_size(SEQ[0]), lax.axis_size(SEQ[1]))
    columns_all = ring_pieces(ring_pieces(down_weight, SEQ[0], outer), SEQ[1], inner_size)
    kept_mask = (1 - erase).astype(jnp.bfloat16)
    erased = inner[None, :, :] * kept_mask[:, :, None]
    row_count = inner.shape[0]
    last_rows = erased[:, row_count - (CONV - 1) :, :]
    prior_rows = from_behind(last_rows, SEQ, 1)
    window = jnp.concatenate([prior_rows, erased], axis=1).astype(jnp.float32)
    convolved = jnp.zeros(erased.shape, jnp.float32)
    for offset in range(CONV):
        convolved = (
            convolved
            + conv_weight[offset] * window[:, CONV - 1 - offset : CONV - 1 - offset + row_count]
        )
    activated = jax.nn.silu(convolved).astype(jnp.bfloat16)
    proj_head = qkv_weight[0]
    head_size = proj_head.shape[0]
    query_key = jnp.einsum(
        "vtd,de->vte", activated, proj_head[:, : 2 * head_size], preferred_element_type=jnp.float32
    )
    queries = query_key[..., :head_size].astype(jnp.bfloat16)
    key_rows = (query_key[..., head_size:] * head_size ** (-0.5)).astype(jnp.bfloat16)
    values = jnp.einsum(
        "vtd,de->vte", erased, proj_head[:, 2 * head_size :], preferred_element_type=jnp.float32
    ).astype(jnp.bfloat16)
    gate_pre = (
        jnp.einsum("vtd,gd->vtg", activated, gate_weight[0], preferred_element_type=jnp.float32)
        + gate_bias[0]
    )
    input_log = 15.0 * jnp.tanh(gate_pre[..., 0] / 15.0)
    forget_log = jax.nn.log_sigmoid(gate_pre[..., 1])
    cumulated = jnp.cumsum(forget_log, axis=1)
    block_decay = cumulated[:, -1]
    key_scale = jnp.exp(block_decay[:, None] - cumulated + input_log)
    scaled_keys = (key_scale[..., None] * key_rows.astype(jnp.float32)).astype(jnp.bfloat16)
    extra = jnp.zeros((EXTRA, head_size), jnp.bfloat16)
    extra = extra.at[0, :3].set(three_parts(block_decay[0]))
    packed = jnp.concatenate([scaled_keys[0], values[0], extra], axis=0)
    gathered = lax.all_gather(packed, SEQ, axis=0, tiled=False)
    block = lax.axis_index(SEQ)
    intra_part = local_terms(queries, key_rows, values, cumulated, input_log)
    numerator = carried_terms(queries, cumulated, gathered, block) + intra_part
    row_mean = jnp.mean(numerator, axis=-1, keepdims=True)
    centred = numerator - row_mean
    row_var = jnp.mean(centred * centred, axis=-1, keepdims=True)
    normed = (centred * lax.rsqrt(row_var + 1e-05) * norm_gain).astype(jnp.bfloat16)
    head_terms = jnp.einsum(
        "vtr,edrc->vtedc", normed, columns_all.reshape(inner_size, outer, head_size, -1),
        preferred_element_type=jnp.float32,
    ).astype(jnp.bfloat16)
    head_terms = jnp.roll(head_terms, lax.axis_index(SEQ[1]) - inner_size // 2, axis=2)
    head_terms = jnp.roll(head_terms, lax.axis_index(SEQ[0]) - outer // 2, axis=3)
    head_terms = jnp.swapaxes(head_terms, 2, 3).reshape(*normed.shape[:2], -1)
    summed = sent_and_summed(head_terms, "head", 2)
    return (residual_in[None, :, :].astype(jnp.float32) + summed).astype(jnp.bfloat16)


def solution(mesh):
    split = Mesh(
        mesh.devices.reshape(4, 8, mesh.shape["head"], mesh.shape["var"]),
        ("seq_0", "seq_1", "head", "var"),
    )
    placed = (
        P(SEQ, "head"),
        P(SEQ, "head"),
        P("var", SEQ),
        P(None, "head"),
        P("head", None, None),
        P("head", None, None),
        P("head", None),
        P("head"),
        P("head", SEQ),
    )
    return jax.shard_map(
        body, mesh=split, in_specs=placed, out_specs=P("var", SEQ, "head"), check_vma=False
    )
```

```python
import jax
import jax.numpy as jnp
from jax import lax
from jax.sharding import Mesh
from jax.sharding import PartitionSpec as P

CONV = 4
SEQ = ("seq_0", "seq_1")
EXTRA = 8


def from_behind(value, axis, steps):
    count = lax.axis_size(axis)
    initial, last = (max(0, -steps), min(count, count - steps))
    return lax.ppermute(value, axis, [(source, source + steps) for source in range(initial, last)])


def split_up(x, dim, size):
    lengths = x.shape
    blocks = x.reshape(*lengths[:dim], size, lengths[dim] // size, *lengths[dim + 1 :])
    return jnp.moveaxis(blocks, dim, 0)


def sent_and_summed(x, axis, dim):
    blocks = split_up(x, dim, lax.axis_size(axis))
    arrived = lax.all_to_all(blocks, axis, split_axis=0, concat_axis=0, tiled=True)
    return arrived.astype(jnp.float32).sum(axis=0)


def ring_pieces(x, axis, count):
    ahead = [(i, (i + 1) % count) for i in range(count)]
    behind = [(i, (i - 1) % count) for i in range(count)]
    before, after = [], []
    forward = backward = x
    for k in range(1, count // 2 + 1):
        forward = lax.ppermute(forward, axis, ahead)
        before.append(forward)
        if k < count - k:
            backward = lax.ppermute(backward, axis, behind)
            after.append(backward)
    return jnp.stack(before[::-1] + [x] + after)


def three_parts(x):
    hi = lax.reduce_precision(x, exponent_bits=8, mantissa_bits=7)
    rest = x - hi
    mid = lax.reduce_precision(rest, exponent_bits=8, mantissa_bits=7)
    lo = rest - mid
    return jnp.stack([hi, mid, lo], axis=-1).astype(jnp.bfloat16)


def local_terms(queries, key_rows, values, cumulated, input_log):
    token_count = queries.shape[1]
    causal = jnp.arange(token_count)[:, None] >= jnp.arange(token_count)[None, :]
    scores = jnp.einsum("vtd,vsd->vts", queries, key_rows, preferred_element_type=jnp.float32)
    exponent = cumulated[:, :, None] - cumulated[:, None, :] + input_log[:, None, :]
    weights = (scores * jnp.exp(jnp.where(causal, exponent, -jnp.inf))).astype(jnp.bfloat16)
    return jnp.einsum("vts,vse->vte", weights, values, preferred_element_type=jnp.float32)


def carried_terms(queries, cumulated, gathered, block):
    blocks, rows, _ = gathered.shape
    token_count = queries.shape[1]
    parts = gathered[:, 2 * token_count, :3].astype(jnp.float32)
    decay = (parts[:, 0] + parts[:, 1]) + parts[:, 2]
    through = jnp.cumsum(decay)
    earlier = jnp.arange(blocks) < block
    before_own = jnp.sum(jnp.where(earlier, decay, 0.0))
    block_exponent = jnp.where(earlier, before_own - through, -jnp.inf)
    scale = jnp.exp(cumulated[:, :, None, None] + block_exponent[None, None, :, None])
    scores = jnp.einsum("vtd,brd->vtbr", queries, gathered, preferred_element_type=jnp.float32)
    weights = scores[..., :token_count] * scale
    weights = jnp.pad(weights, ((0, 0), (0, 0), (0, 0), (token_count, rows - 2 * token_count)))
    high = weights.astype(jnp.bfloat16)
    low = (weights - high.astype(jnp.float32)).astype(jnp.bfloat16)
    return jnp.einsum("vtbr,bre->vte", high, gathered, preferred_element_type=jnp.float32) + jnp.einsum(
        "vtbr,bre->vte", low, gathered, preferred_element_type=jnp.float32
    )


def body(
    inner,
    residual_in,
    erase,
    conv_weight,
    qkv_weight,
    gate_weight,
    gate_bias,
    norm_gain,
    down_weight,
):
    outer, inner_size = (lax.axis_size(SEQ[0]), lax.axis_size(SEQ[1]))
    columns_all = ring_pieces(ring_pieces(down_weight, SEQ[0], outer), SEQ[1], inner_size)
    kept_mask = (1 - erase).astype(jnp.bfloat16)
    erased = inner[None, :, :] * kept_mask[:, :, None]
    row_count = inner.shape[0]
    last_rows = erased[:, row_count - (CONV - 1) :, :]
    prior_rows = from_behind(last_rows, SEQ, 1)
    window = jnp.concatenate([prior_rows, erased], axis=1).astype(jnp.float32)
    convolved = jnp.zeros(erased.shape, jnp.float32)
    for offset in range(CONV):
        convolved = (
            convolved
            + conv_weight[offset] * window[:, CONV - 1 - offset : CONV - 1 - offset + row_count]
        )
    activated = jax.nn.silu(convolved).astype(jnp.bfloat16)
    proj_head = qkv_weight[0]
    head_size = proj_head.shape[0]
    query_key = jnp.einsum(
        "vtd,de->vte", activated, proj_head[:, : 2 * head_size], preferred_element_type=jnp.float32
    )
    queries = query_key[..., :head_size].astype(jnp.bfloat16)
    key_rows = (query_key[..., head_size:] * head_size ** (-0.5)).astype(jnp.bfloat16)
    values = jnp.einsum(
        "vtd,de->vte", erased, proj_head[:, 2 * head_size :], preferred_element_type=jnp.float32
    ).astype(jnp.bfloat16)
    gate_pre = (
        jnp.einsum("vtd,gd->vtg", activated, gate_weight[0], preferred_element_type=jnp.float32)
        + gate_bias[0]
    )
    input_log = 15.0 * jnp.tanh(gate_pre[..., 0] / 15.0)
    forget_log = jax.nn.log_sigmoid(gate_pre[..., 1])
    cumulated = jnp.cumsum(forget_log, axis=1)
    block_decay = cumulated[:, -1]
    key_scale = jnp.exp(block_decay[:, None] - cumulated + input_log)
    scaled_keys = (key_scale[..., None] * key_rows.astype(jnp.float32)).astype(jnp.bfloat16)
    extra = jnp.zeros((EXTRA, head_size), jnp.bfloat16)
    extra = extra.at[0, :3].set(three_parts(block_decay[0]))
    packed = jnp.concatenate([scaled_keys[0], values[0], extra], axis=0)
    gathered = lax.all_gather(packed, SEQ[1], axis=0, tiled=False)
    gathered = lax.all_gather(gathered, SEQ[0], axis=0, tiled=False)
    gathered = gathered.reshape(-1, *packed.shape)
    block = lax.axis_index(SEQ)
    intra_part = local_terms(queries, key_rows, values, cumulated, input_log)
    numerator = carried_terms(queries, cumulated, gathered, block) + intra_part
    row_mean = jnp.mean(numerator, axis=-1, keepdims=True)
    centred = numerator - row_mean
    row_var = jnp.mean(centred * centred, axis=-1, keepdims=True)
    normed = (centred * lax.rsqrt(row_var + 1e-05) * norm_gain).astype(jnp.bfloat16)
    head_terms = jnp.einsum(
        "vtr,edrc->vtedc", normed, columns_all.reshape(inner_size, outer, head_size, -1),
        preferred_element_type=jnp.float32,
    ).astype(jnp.bfloat16)
    head_terms = jnp.roll(head_terms, lax.axis_index(SEQ[1]) - inner_size // 2, axis=2)
    head_terms = jnp.roll(head_terms, lax.axis_index(SEQ[0]) - outer // 2, axis=3)
    head_terms = jnp.swapaxes(head_terms, 2, 3).reshape(*normed.shape[:2], -1)
    summed = sent_and_summed(head_terms, "head", 2)
    return (residual_in[None, :, :].astype(jnp.float32) + summed).astype(jnp.bfloat16)


def solution(mesh):
    split = Mesh(
        mesh.devices.reshape(4, 8, mesh.shape["head"], mesh.shape["var"]),
        ("seq_0", "seq_1", "head", "var"),
    )
    placed = (
        P(SEQ, "head"),
        P(SEQ, "head"),
        P("var", SEQ),
        P(None, "head"),
        P("head", None, None),
        P("head", None, None),
        P("head", None),
        P("head"),
        P("head", SEQ),
    )
    return jax.shard_map(
        body, mesh=split, in_specs=placed, out_specs=P("var", SEQ, "head"), check_vma=False
    )
```

```python
import jax
import jax.numpy as jnp
from jax import lax
from jax.sharding import Mesh
from jax.sharding import PartitionSpec as P

CONV = 4
SEQ = ("seq_0", "seq_1")
HEAD = ("head_1", "head_0")
EXTRA = 16


def from_behind(value, axis, steps):
    count = lax.axis_size(axis)
    initial, last = (max(0, -steps), min(count, count - steps))
    return lax.ppermute(value, axis, [(source, source + steps) for source in range(initial, last)])


def split_up(x, dim, size):
    lengths = x.shape
    blocks = x.reshape(*lengths[:dim], size, lengths[dim] // size, *lengths[dim + 1 :])
    return jnp.moveaxis(blocks, dim, 0)


def sent_and_summed(x, axis, dim):
    blocks = split_up(x, dim, lax.axis_size(axis))
    arrived = lax.all_to_all(blocks, axis, split_axis=0, concat_axis=0, tiled=True)
    return arrived.astype(jnp.float32).sum(axis=0)


def ring_pieces(x, axis, count):
    ahead = [(i, (i + 1) % count) for i in range(count)]
    behind = [(i, (i - 1) % count) for i in range(count)]
    before, after = [], []
    forward = backward = x
    for k in range(1, count // 2 + 1):
        forward = lax.ppermute(forward, axis, ahead)
        before.append(forward)
        if k < count - k:
            backward = lax.ppermute(backward, axis, behind)
            after.append(backward)
    return jnp.stack(before[::-1] + [x] + after)


def three_parts(x):
    hi = lax.reduce_precision(x, exponent_bits=8, mantissa_bits=7)
    rest = x - hi
    mid = lax.reduce_precision(rest, exponent_bits=8, mantissa_bits=7)
    lo = rest - mid
    return jnp.stack([hi, mid, lo], axis=-1).astype(jnp.bfloat16)


def local_terms(queries, key_rows, values, cumulated, input_log):
    token_count = queries.shape[1]
    causal = jnp.arange(token_count)[:, None] >= jnp.arange(token_count)[None, :]
    scores = jnp.einsum("vtd,vsd->vts", queries, key_rows, preferred_element_type=jnp.float32)
    exponent = cumulated[:, :, None] - cumulated[:, None, :] + input_log[:, None, :]
    weights = (scores * jnp.exp(jnp.where(causal, exponent, -jnp.inf))).astype(jnp.bfloat16)
    return jnp.einsum("vts,vse->vte", weights, values, preferred_element_type=jnp.float32)


def carried_terms(queries, cumulated, gathered, block):
    blocks, rows, head_size = gathered.shape
    token_count = queries.shape[1]
    keys_all = gathered[:, :token_count, :].reshape(blocks * token_count, head_size)
    values_all = gathered[:, token_count : 2 * token_count, :].reshape(blocks * token_count, head_size)
    parts = gathered[:, 2 * token_count, :3].astype(jnp.float32)
    decay = (parts[:, 0] + parts[:, 1]) + parts[:, 2]
    through = jnp.cumsum(decay)
    before_own = jnp.sum(jnp.where(jnp.arange(blocks) < block, decay, 0.0))
    earlier = jnp.arange(blocks) < block
    block_exponent = jnp.where(earlier, before_own - through, -jnp.inf)
    exponent = cumulated[:, :, None, None] + block_exponent[None, None, :, None]
    scale = jnp.exp(jnp.broadcast_to(exponent, (*cumulated.shape, blocks, token_count)))
    scale = scale.reshape(*cumulated.shape, blocks * token_count)
    scores = jnp.einsum("vtd,sd->vts", queries, keys_all, preferred_element_type=jnp.float32)
    weights = scores * scale
    high = weights.astype(jnp.bfloat16)
    low = (weights - high.astype(jnp.float32)).astype(jnp.bfloat16)
    return jnp.einsum("vts,se->vte", high, values_all, preferred_element_type=jnp.float32) + jnp.einsum(
        "vts,se->vte", low, values_all, preferred_element_type=jnp.float32
    )


def body(
    inner,
    residual_in,
    erase,
    conv_weight,
    qkv_weight,
    gate_weight,
    gate_bias,
    norm_gain,
    down_weight,
):
    outer, inner_size = (lax.axis_size(SEQ[0]), lax.axis_size(SEQ[1]))
    columns_all = ring_pieces(ring_pieces(down_weight, SEQ[0], outer), SEQ[1], inner_size)
    kept_mask = (1 - erase).astype(jnp.bfloat16)
    erased = inner[None, :, :] * kept_mask[:, :, None]
    row_count = inner.shape[0]
    last_rows = erased[:, row_count - (CONV - 1) :, :]
    prior_rows = from_behind(last_rows, SEQ, 1)
    window = jnp.concatenate([prior_rows, erased], axis=1).astype(jnp.float32)
    convolved = jnp.zeros(erased.shape, jnp.float32)
    for offset in range(CONV):
        convolved = (
            convolved
            + conv_weight[offset] * window[:, CONV - 1 - offset : CONV - 1 - offset + row_count]
        )
    activated = jax.nn.silu(convolved).astype(jnp.bfloat16)
    proj_head = qkv_weight[0]
    head_size = proj_head.shape[0]
    query_key = jnp.einsum(
        "vtd,de->vte", activated, proj_head[:, : 2 * head_size], preferred_element_type=jnp.float32
    )
    queries = query_key[..., :head_size].astype(jnp.bfloat16)
    key_rows = (query_key[..., head_size:] * head_size ** (-0.5)).astype(jnp.bfloat16)
    values = jnp.einsum(
        "vtd,de->vte", erased, proj_head[:, 2 * head_size :], preferred_element_type=jnp.float32
    ).astype(jnp.bfloat16)
    gate_pre = (
        jnp.einsum("vtd,gd->vtg", activated, gate_weight[0], preferred_element_type=jnp.float32)
        + gate_bias[0]
    )
    input_log = 15.0 * jnp.tanh(gate_pre[..., 0] / 15.0)
    forget_log = jax.nn.log_sigmoid(gate_pre[..., 1])
    cumulated = jnp.cumsum(forget_log, axis=1)
    block_decay = cumulated[:, -1]
    key_scale = jnp.exp(block_decay[:, None] - cumulated + input_log)
    scaled_keys = (key_scale[..., None] * key_rows.astype(jnp.float32)).astype(jnp.bfloat16)
    extra = jnp.zeros((EXTRA, head_size), jnp.bfloat16)
    extra = extra.at[0, :3].set(three_parts(block_decay[0]))
    packed = jnp.concatenate([scaled_keys[0], values[0], extra], axis=0)
    gathered = lax.all_gather(packed, SEQ, axis=0, tiled=False)
    block = lax.axis_index(SEQ)
    intra_part = local_terms(queries, key_rows, values, cumulated, input_log)
    numerator = carried_terms(queries, cumulated, gathered, block) + intra_part
    row_mean = jnp.mean(numerator, axis=-1, keepdims=True)
    centred = numerator - row_mean
    row_var = jnp.mean(centred * centred, axis=-1, keepdims=True)
    normed = (centred * lax.rsqrt(row_var + 1e-05) * norm_gain).astype(jnp.bfloat16)
    head_terms = jnp.einsum(
        "vtr,edrc->vtedc", normed, columns_all.reshape(inner_size, outer, head_size, -1),
        preferred_element_type=jnp.float32,
    ).astype(jnp.bfloat16)
    head_terms = jnp.roll(head_terms, lax.axis_index(SEQ[1]) - inner_size // 2, axis=2)
    head_terms = jnp.roll(head_terms, lax.axis_index(SEQ[0]) - outer // 2, axis=3)
    head_terms = jnp.swapaxes(head_terms, 2, 3).reshape(*normed.shape[:2], -1)
    pair, across = HEAD
    blocks = head_terms.reshape(*head_terms.shape[:2], lax.axis_size(across), lax.axis_size(pair), -1)
    arrived = lax.all_to_all(blocks, pair, split_axis=3, concat_axis=3, tiled=True)
    pair_sum = jnp.sum(arrived.astype(jnp.float32), axis=3).astype(jnp.bfloat16)
    summed = lax.all_to_all(pair_sum, across, split_axis=2, concat_axis=2, tiled=True)
    summed = jnp.sum(summed.astype(jnp.float32), axis=2)
    return (residual_in[None, :, :].astype(jnp.float32) + summed).astype(jnp.bfloat16)


def solution(mesh):
    split = Mesh(
        mesh.devices.reshape(4, 8, mesh.shape["head"] // 2, 2, mesh.shape["var"]),
        ("seq_0", "seq_1", "head_0", "head_1", "var"),
    )
    heads = HEAD[::-1]
    placed = (
        P(SEQ, heads),
        P(SEQ, heads),
        P("var", SEQ),
        P(None, heads),
        P(heads, None, None),
        P(heads, None, None),
        P(heads, None),
        P(heads),
        P(heads, SEQ),
    )
    return jax.shard_map(
        body, mesh=split, in_specs=placed, out_specs=P("var", SEQ, heads), check_vma=False
    )
```

```python
import jax
import jax.numpy as jnp
from jax import lax
from jax.sharding import Mesh
from jax.sharding import PartitionSpec as P

CONV = 4
SEQ = ("seq_0", "seq_1")
HEAD = ("head_1", "head_0")
EXTRA = 8


def from_behind(value, axis, steps):
    count = lax.axis_size(axis)
    initial, last = (max(0, -steps), min(count, count - steps))
    return lax.ppermute(value, axis, [(source, source + steps) for source in range(initial, last)])


def split_up(x, dim, size):
    lengths = x.shape
    blocks = x.reshape(*lengths[:dim], size, lengths[dim] // size, *lengths[dim + 1 :])
    return jnp.moveaxis(blocks, dim, 0)


def sent_and_summed(x, axis, dim):
    blocks = split_up(x, dim, lax.axis_size(axis))
    arrived = lax.all_to_all(blocks, axis, split_axis=0, concat_axis=0, tiled=True)
    return arrived.astype(jnp.float32).sum(axis=0)


def ring_pieces(x, axis, count):
    ahead = [(i, (i + 1) % count) for i in range(count)]
    behind = [(i, (i - 1) % count) for i in range(count)]
    before, after = [], []
    forward = backward = x
    for k in range(1, count // 2 + 1):
        forward = lax.ppermute(forward, axis, ahead)
        before.append(forward)
        if k < count - k:
            backward = lax.ppermute(backward, axis, behind)
            after.append(backward)
    return jnp.stack(before[::-1] + [x] + after)


def three_parts(x):
    hi = lax.reduce_precision(x, exponent_bits=8, mantissa_bits=7)
    rest = x - hi
    mid = lax.reduce_precision(rest, exponent_bits=8, mantissa_bits=7)
    lo = rest - mid
    return jnp.stack([hi, mid, lo], axis=-1).astype(jnp.bfloat16)


def local_terms(queries, key_rows, values, cumulated, input_log):
    token_count = queries.shape[1]
    causal = jnp.arange(token_count)[:, None] >= jnp.arange(token_count)[None, :]
    scores = jnp.einsum("vtd,vsd->vts", queries, key_rows, preferred_element_type=jnp.float32)
    exponent = cumulated[:, :, None] - cumulated[:, None, :] + input_log[:, None, :]
    weights = (scores * jnp.exp(jnp.where(causal, exponent, -jnp.inf))).astype(jnp.bfloat16)
    return jnp.einsum("vts,vse->vte", weights, values, preferred_element_type=jnp.float32)


def carried_terms(queries, cumulated, gathered, values_ring, block, outer, inner_size):
    blocks = gathered.shape[0]
    token_count = queries.shape[1]
    keys_all = gathered[:, :token_count, :]
    parts = gathered[:, token_count, :3].astype(jnp.float32)
    decay = (parts[:, 0] + parts[:, 1]) + parts[:, 2]
    through = jnp.cumsum(decay)
    earlier = jnp.arange(blocks) < block
    before_own = jnp.sum(jnp.where(earlier, decay, 0.0))
    block_exponent = jnp.where(earlier, before_own - through, -jnp.inf)
    scale = jnp.exp(cumulated[:, :, None, None] + block_exponent[None, None, :, None])
    scores = jnp.einsum("vtd,bsd->vtbs", queries, keys_all, preferred_element_type=jnp.float32)
    weights = (scores * scale).reshape(*queries.shape[:2], outer, inner_size, token_count)
    weights = jnp.roll(weights, outer // 2 - lax.axis_index(SEQ[0]), axis=2)
    weights = jnp.roll(weights, inner_size // 2 - lax.axis_index(SEQ[1]), axis=3)
    high = weights.astype(jnp.bfloat16)
    low = (weights - high.astype(jnp.float32)).astype(jnp.bfloat16)
    return jnp.einsum("vtqps,pqse->vte", high, values_ring, preferred_element_type=jnp.float32) + jnp.einsum(
        "vtqps,pqse->vte", low, values_ring, preferred_element_type=jnp.float32
    )


def body(
    inner,
    residual_in,
    erase,
    conv_weight,
    qkv_weight,
    gate_weight,
    gate_bias,
    norm_gain,
    down_weight,
):
    outer, inner_size = (lax.axis_size(SEQ[0]), lax.axis_size(SEQ[1]))
    columns_all = ring_pieces(ring_pieces(down_weight, SEQ[0], outer), SEQ[1], inner_size)
    kept_mask = (1 - erase).astype(jnp.bfloat16)
    erased = inner[None, :, :] * kept_mask[:, :, None]
    row_count = inner.shape[0]
    last_rows = erased[:, row_count - (CONV - 1) :, :]
    prior_rows = from_behind(last_rows, SEQ, 1)
    window = jnp.concatenate([prior_rows, erased], axis=1).astype(jnp.float32)
    convolved = jnp.zeros(erased.shape, jnp.float32)
    for offset in range(CONV):
        convolved = (
            convolved
            + conv_weight[offset] * window[:, CONV - 1 - offset : CONV - 1 - offset + row_count]
        )
    activated = jax.nn.silu(convolved).astype(jnp.bfloat16)
    proj_head = qkv_weight[0]
    head_size = proj_head.shape[0]
    query_key = jnp.einsum(
        "vtd,de->vte", activated, proj_head[:, : 2 * head_size], preferred_element_type=jnp.float32
    )
    queries = query_key[..., :head_size].astype(jnp.bfloat16)
    key_rows = (query_key[..., head_size:] * head_size ** (-0.5)).astype(jnp.bfloat16)
    values = jnp.einsum(
        "vtd,de->vte", erased, proj_head[:, 2 * head_size :], preferred_element_type=jnp.float32
    ).astype(jnp.bfloat16)
    gate_pre = (
        jnp.einsum("vtd,gd->vtg", activated, gate_weight[0], preferred_element_type=jnp.float32)
        + gate_bias[0]
    )
    input_log = 15.0 * jnp.tanh(gate_pre[..., 0] / 15.0)
    forget_log = jax.nn.log_sigmoid(gate_pre[..., 1])
    cumulated = jnp.cumsum(forget_log, axis=1)
    block_decay = cumulated[:, -1]
    key_scale = jnp.exp(block_decay[:, None] - cumulated + input_log)
    scaled_keys = (key_scale[..., None] * key_rows.astype(jnp.float32)).astype(jnp.bfloat16)
    extra = jnp.zeros((EXTRA, head_size), jnp.bfloat16)
    extra = extra.at[0, :3].set(three_parts(block_decay[0]))
    packed = jnp.concatenate([scaled_keys[0], extra], axis=0)
    gathered = lax.all_gather(packed, SEQ, axis=0, tiled=False)
    values_ring = ring_pieces(ring_pieces(values[0], SEQ[0], outer), SEQ[1], inner_size)
    block = lax.axis_index(SEQ)
    intra_part = local_terms(queries, key_rows, values, cumulated, input_log)
    numerator = carried_terms(queries, cumulated, gathered, values_ring, block, outer, inner_size) + intra_part
    row_mean = jnp.mean(numerator, axis=-1, keepdims=True)
    centred = numerator - row_mean
    row_var = jnp.mean(centred * centred, axis=-1, keepdims=True)
    normed = (centred * lax.rsqrt(row_var + 1e-05) * norm_gain).astype(jnp.bfloat16)
    head_terms = jnp.einsum(
        "vtr,edrc->vtedc", normed, columns_all.reshape(inner_size, outer, head_size, -1),
        preferred_element_type=jnp.float32,
    ).astype(jnp.bfloat16)
    head_terms = jnp.roll(head_terms, lax.axis_index(SEQ[1]) - inner_size // 2, axis=2)
    head_terms = jnp.roll(head_terms, lax.axis_index(SEQ[0]) - outer // 2, axis=3)
    head_terms = jnp.swapaxes(head_terms, 2, 3).reshape(*normed.shape[:2], -1)
    pair, across = HEAD
    blocks = head_terms.reshape(*head_terms.shape[:2], lax.axis_size(across), lax.axis_size(pair), -1)
    arrived = lax.all_to_all(blocks, pair, split_axis=3, concat_axis=3, tiled=True)
    pair_sum = jnp.sum(arrived.astype(jnp.float32), axis=3).astype(jnp.bfloat16)
    summed = lax.all_to_all(pair_sum, across, split_axis=2, concat_axis=2, tiled=True)
    summed = jnp.sum(summed.astype(jnp.float32), axis=2)
    return (residual_in[None, :, :].astype(jnp.float32) + summed).astype(jnp.bfloat16)


def solution(mesh):
    split = Mesh(
        mesh.devices.reshape(4, 8, mesh.shape["head"] // 2, 2, mesh.shape["var"]),
        ("seq_0", "seq_1", "head_0", "head_1", "var"),
    )
    heads = HEAD[::-1]
    placed = (
        P(SEQ, heads),
        P(SEQ, heads),
        P("var", SEQ),
        P(None, heads),
        P(heads, None, None),
        P(heads, None, None),
        P(heads, None),
        P(heads),
        P(heads, SEQ),
    )
    return jax.shard_map(
        body, mesh=split, in_specs=placed, out_specs=P("var", SEQ, heads), check_vma=False
    )
```

```python
import jax
import jax.numpy as jnp
from jax import lax
from jax.sharding import Mesh
from jax.sharding import PartitionSpec as P

CONV = 4
SEQ = ("seq_0", "seq_1")
HEAD = ("head_1", "head_0")
EXTRA = 16


def from_behind(value, axis, steps):
    count = lax.axis_size(axis)
    initial, last = (max(0, -steps), min(count, count - steps))
    return lax.ppermute(value, axis, [(source, source + steps) for source in range(initial, last)])


def split_up(x, dim, size):
    lengths = x.shape
    blocks = x.reshape(*lengths[:dim], size, lengths[dim] // size, *lengths[dim + 1 :])
    return jnp.moveaxis(blocks, dim, 0)


def sent_and_summed(x, axis, dim):
    blocks = split_up(x, dim, lax.axis_size(axis))
    arrived = lax.all_to_all(blocks, axis, split_axis=0, concat_axis=0, tiled=True)
    return arrived.astype(jnp.float32).sum(axis=0)


def ring_pieces(x, axis, count):
    ahead = [(i, (i + 1) % count) for i in range(count)]
    behind = [(i, (i - 1) % count) for i in range(count)]
    before, after = [], []
    forward = backward = x
    for k in range(1, count // 2 + 1):
        forward = lax.ppermute(forward, axis, ahead)
        before.append(forward)
        if k < count - k:
            backward = lax.ppermute(backward, axis, behind)
            after.append(backward)
    return jnp.stack(before[::-1] + [x] + after)


def three_parts(x):
    hi = lax.reduce_precision(x, exponent_bits=8, mantissa_bits=7)
    rest = x - hi
    mid = lax.reduce_precision(rest, exponent_bits=8, mantissa_bits=7)
    lo = rest - mid
    return jnp.stack([hi, mid, lo], axis=-1).astype(jnp.bfloat16)


def local_terms(queries, key_rows, values, cumulated, input_log):
    token_count = queries.shape[1]
    causal = jnp.arange(token_count)[:, None] >= jnp.arange(token_count)[None, :]
    scores = jnp.einsum("vtd,vsd->vts", queries, key_rows, preferred_element_type=jnp.float32)
    exponent = cumulated[:, :, None] - cumulated[:, None, :] + input_log[:, None, :]
    weights = (scores * jnp.exp(jnp.where(causal, exponent, -jnp.inf))).astype(jnp.bfloat16)
    return jnp.einsum("vts,vse->vte", weights, values, preferred_element_type=jnp.float32)


def carried_terms(queries, cumulated, gathered, block):
    blocks, rows, head_size = gathered.shape
    token_count = queries.shape[1]
    keys_all = gathered[:, :token_count, :].reshape(blocks * token_count, head_size)
    values_all = gathered[:, token_count : 2 * token_count, :].reshape(blocks * token_count, head_size)
    parts = gathered[:, 2 * token_count, :3].astype(jnp.float32)
    decay = (parts[:, 0] + parts[:, 1]) + parts[:, 2]
    outer, inner_size = (lax.axis_size(SEQ[0]), lax.axis_size(SEQ[1]))
    decay = decay.reshape(inner_size, outer).T.reshape(-1)
    through = jnp.cumsum(decay)
    before_own = jnp.sum(jnp.where(jnp.arange(blocks) < block, decay, 0.0))
    earlier = jnp.arange(blocks) < block
    block_exponent = jnp.where(earlier, before_own - through, -jnp.inf)
    block_exponent = block_exponent.reshape(outer, inner_size).T.reshape(-1)
    exponent = cumulated[:, :, None, None] + block_exponent[None, None, :, None]
    scale = jnp.exp(jnp.broadcast_to(exponent, (*cumulated.shape, blocks, token_count)))
    scale = scale.reshape(*cumulated.shape, blocks * token_count)
    scores = jnp.einsum("vtd,sd->vts", queries, keys_all, preferred_element_type=jnp.float32)
    weights = scores * scale
    high = weights.astype(jnp.bfloat16)
    low = (weights - high.astype(jnp.float32)).astype(jnp.bfloat16)
    return jnp.einsum("vts,se->vte", high, values_all, preferred_element_type=jnp.float32) + jnp.einsum(
        "vts,se->vte", low, values_all, preferred_element_type=jnp.float32
    )


def body(
    inner,
    residual_in,
    erase,
    conv_weight,
    qkv_weight,
    gate_weight,
    gate_bias,
    norm_gain,
    down_weight,
):
    outer, inner_size = (lax.axis_size(SEQ[0]), lax.axis_size(SEQ[1]))
    columns_all = ring_pieces(ring_pieces(down_weight, SEQ[0], outer), SEQ[1], inner_size)
    kept_mask = (1 - erase).astype(jnp.bfloat16)
    erased = inner[None, :, :] * kept_mask[:, :, None]
    row_count = inner.shape[0]
    last_rows = erased[:, row_count - (CONV - 1) :, :]
    prior_rows = from_behind(last_rows, SEQ, 1)
    window = jnp.concatenate([prior_rows, erased], axis=1).astype(jnp.float32)
    convolved = jnp.zeros(erased.shape, jnp.float32)
    for offset in range(CONV):
        convolved = (
            convolved
            + conv_weight[offset] * window[:, CONV - 1 - offset : CONV - 1 - offset + row_count]
        )
    activated = jax.nn.silu(convolved).astype(jnp.bfloat16)
    proj_head = qkv_weight[0]
    head_size = proj_head.shape[0]
    query_key = jnp.einsum(
        "vtd,de->vte", activated, proj_head[:, : 2 * head_size], preferred_element_type=jnp.float32
    )
    queries = query_key[..., :head_size].astype(jnp.bfloat16)
    key_rows = (query_key[..., head_size:] * head_size ** (-0.5)).astype(jnp.bfloat16)
    values = jnp.einsum(
        "vtd,de->vte", erased, proj_head[:, 2 * head_size :], preferred_element_type=jnp.float32
    ).astype(jnp.bfloat16)
    gate_pre = (
        jnp.einsum("vtd,gd->vtg", activated, gate_weight[0], preferred_element_type=jnp.float32)
        + gate_bias[0]
    )
    input_log = 15.0 * jnp.tanh(gate_pre[..., 0] / 15.0)
    forget_log = jax.nn.log_sigmoid(gate_pre[..., 1])
    cumulated = jnp.cumsum(forget_log, axis=1)
    block_decay = cumulated[:, -1]
    key_scale = jnp.exp(block_decay[:, None] - cumulated + input_log)
    scaled_keys = (key_scale[..., None] * key_rows.astype(jnp.float32)).astype(jnp.bfloat16)
    extra = jnp.zeros((EXTRA, head_size), jnp.bfloat16)
    extra = extra.at[0, :3].set(three_parts(block_decay[0]))
    packed = jnp.concatenate([scaled_keys[0], values[0], extra], axis=0)
    gathered = lax.all_gather(packed, SEQ[0], axis=0, tiled=False)
    gathered = lax.all_gather(gathered, SEQ[1], axis=0, tiled=False).reshape(-1, *packed.shape)
    block = lax.axis_index(SEQ)
    intra_part = local_terms(queries, key_rows, values, cumulated, input_log)
    numerator = carried_terms(queries, cumulated, gathered, block) + intra_part
    row_mean = jnp.mean(numerator, axis=-1, keepdims=True)
    centred = numerator - row_mean
    row_var = jnp.mean(centred * centred, axis=-1, keepdims=True)
    normed = (centred * lax.rsqrt(row_var + 1e-05) * norm_gain).astype(jnp.bfloat16)
    head_terms = jnp.einsum(
        "vtr,edrc->vtedc", normed, columns_all.reshape(inner_size, outer, head_size, -1),
        preferred_element_type=jnp.float32,
    ).astype(jnp.bfloat16)
    head_terms = jnp.roll(head_terms, lax.axis_index(SEQ[1]) - inner_size // 2, axis=2)
    head_terms = jnp.roll(head_terms, lax.axis_index(SEQ[0]) - outer // 2, axis=3)
    head_terms = jnp.swapaxes(head_terms, 2, 3).reshape(*normed.shape[:2], -1)
    pair, across = HEAD
    blocks = head_terms.reshape(*head_terms.shape[:2], lax.axis_size(across), lax.axis_size(pair), -1)
    arrived = lax.all_to_all(blocks, pair, split_axis=3, concat_axis=3, tiled=True)
    pair_sum = jnp.sum(arrived.astype(jnp.float32), axis=3).astype(jnp.bfloat16)
    summed = lax.all_to_all(pair_sum, across, split_axis=2, concat_axis=2, tiled=True)
    summed = jnp.sum(summed.astype(jnp.float32), axis=2)
    return (residual_in[None, :, :].astype(jnp.float32) + summed).astype(jnp.bfloat16)


def solution(mesh):
    split = Mesh(
        mesh.devices.reshape(4, 8, mesh.shape["head"] // 2, 2, mesh.shape["var"]),
        ("seq_0", "seq_1", "head_0", "head_1", "var"),
    )
    heads = HEAD[::-1]
    placed = (
        P(SEQ, heads),
        P(SEQ, heads),
        P("var", SEQ),
        P(None, heads),
        P(heads, None, None),
        P(heads, None, None),
        P(heads, None),
        P(heads),
        P(heads, SEQ),
    )
    return jax.shard_map(
        body, mesh=split, in_specs=placed, out_specs=P("var", SEQ, heads), check_vma=False
    )
```

```python
import jax
import jax.numpy as jnp
from jax import lax
from jax.sharding import Mesh
from jax.sharding import PartitionSpec as P

CONV = 4
SEQ = ("seq_0", "seq_1")
HEAD = ("head_1", "head_0")
EXTRA = 16


def from_behind(value, axis, steps):
    count = lax.axis_size(axis)
    initial, last = (max(0, -steps), min(count, count - steps))
    return lax.ppermute(value, axis, [(source, source + steps) for source in range(initial, last)])


def split_up(x, dim, size):
    lengths = x.shape
    blocks = x.reshape(*lengths[:dim], size, lengths[dim] // size, *lengths[dim + 1 :])
    return jnp.moveaxis(blocks, dim, 0)


def sent_and_summed(x, axis, dim):
    blocks = split_up(x, dim, lax.axis_size(axis))
    arrived = lax.all_to_all(blocks, axis, split_axis=0, concat_axis=0, tiled=True)
    return arrived.astype(jnp.float32).sum(axis=0)


def ring_pieces(x, axis, count):
    ahead = [(i, (i + 1) % count) for i in range(count)]
    behind = [(i, (i - 1) % count) for i in range(count)]
    before, after = [], []
    forward = backward = x
    for k in range(1, count // 2 + 1):
        forward = lax.ppermute(forward, axis, ahead)
        before.append(forward)
        if k < count - k:
            backward = lax.ppermute(backward, axis, behind)
            after.append(backward)
    return jnp.stack(before[::-1] + [x] + after)


def three_parts(x):
    hi = lax.reduce_precision(x, exponent_bits=8, mantissa_bits=7)
    rest = x - hi
    mid = lax.reduce_precision(rest, exponent_bits=8, mantissa_bits=7)
    lo = rest - mid
    return jnp.stack([hi, mid, lo], axis=-1).astype(jnp.bfloat16)


def local_terms(queries, key_rows, values, cumulated, input_log):
    token_count = queries.shape[1]
    causal = jnp.arange(token_count)[:, None] >= jnp.arange(token_count)[None, :]
    scores = jnp.einsum("vtd,vsd->vts", queries, key_rows, preferred_element_type=jnp.float32)
    exponent = cumulated[:, :, None] - cumulated[:, None, :] + input_log[:, None, :]
    weights = (scores * jnp.exp(jnp.where(causal, exponent, -jnp.inf))).astype(jnp.bfloat16)
    return jnp.einsum("vts,vse->vte", weights, values, preferred_element_type=jnp.float32)


def carried_terms(queries, cumulated, gathered, block):
    blocks, rows, head_size = gathered.shape
    token_count = queries.shape[1]
    keys_all = gathered[:, :token_count, :].reshape(blocks * token_count, head_size)
    values_all = gathered[:, token_count : 2 * token_count, :].reshape(blocks * token_count, head_size)
    parts = gathered[:, 2 * token_count, :3].astype(jnp.float32)
    decay = (parts[:, 0] + parts[:, 1]) + parts[:, 2]
    through = jnp.cumsum(decay)
    before_own = jnp.sum(jnp.where(jnp.arange(blocks) < block, decay, 0.0))
    earlier = jnp.arange(blocks) < block
    block_exponent = jnp.where(earlier, before_own - through, -jnp.inf)
    scale = jnp.exp(cumulated[:, :, None] + block_exponent[None, None, :])
    scores = jnp.einsum("vtd,sd->vts", queries, keys_all, preferred_element_type=jnp.float32)
    scores = scores.reshape(*cumulated.shape, blocks, token_count) * scale[..., None]
    weights = scores.reshape(*cumulated.shape, blocks * token_count).astype(jnp.bfloat16)
    return jnp.einsum("vts,se->vte", weights, values_all, preferred_element_type=jnp.float32)


def body(
    inner,
    residual_in,
    erase,
    conv_weight,
    qkv_weight,
    gate_weight,
    gate_bias,
    norm_gain,
    down_weight,
):
    outer, inner_size = (lax.axis_size(SEQ[0]), lax.axis_size(SEQ[1]))
    columns_all = ring_pieces(ring_pieces(down_weight, SEQ[0], outer), SEQ[1], inner_size)
    kept_mask = (1 - erase).astype(jnp.bfloat16)
    erased = inner[None, :, :] * kept_mask[:, :, None]
    row_count = inner.shape[0]
    last_rows = erased[:, row_count - (CONV - 1) :, :]
    prior_rows = from_behind(last_rows, SEQ, 1)
    window = jnp.concatenate([prior_rows, erased], axis=1).astype(jnp.float32)
    convolved = jnp.zeros(erased.shape, jnp.float32)
    for offset in range(CONV):
        convolved = (
            convolved
            + conv_weight[offset] * window[:, CONV - 1 - offset : CONV - 1 - offset + row_count]
        )
    activated = jax.nn.silu(convolved).astype(jnp.bfloat16)
    proj_head = qkv_weight[0]
    head_size = proj_head.shape[0]
    query_key = jnp.einsum(
        "vtd,de->vte", activated, proj_head[:, : 2 * head_size], preferred_element_type=jnp.float32
    )
    queries = query_key[..., :head_size].astype(jnp.bfloat16)
    key_rows = (query_key[..., head_size:] * head_size ** (-0.5)).astype(jnp.bfloat16)
    values = jnp.einsum(
        "vtd,de->vte", erased, proj_head[:, 2 * head_size :], preferred_element_type=jnp.float32
    ).astype(jnp.bfloat16)
    gate_pre = (
        jnp.einsum("vtd,gd->vtg", activated, gate_weight[0], preferred_element_type=jnp.float32)
        + gate_bias[0]
    )
    input_log = 15.0 * jnp.tanh(gate_pre[..., 0] / 15.0)
    forget_log = jax.nn.log_sigmoid(gate_pre[..., 1])
    cumulated = jnp.cumsum(forget_log, axis=1)
    block_decay = cumulated[:, -1]
    key_scale = jnp.exp(block_decay[:, None] - cumulated + input_log)
    scaled_keys = (key_scale[..., None] * key_rows.astype(jnp.float32)).astype(jnp.bfloat16)
    extra = jnp.zeros((EXTRA, head_size), jnp.bfloat16)
    extra = extra.at[0, :3].set(three_parts(block_decay[0]))
    packed = jnp.concatenate([scaled_keys[0], values[0], extra], axis=0)
    gathered = lax.all_gather(packed, SEQ, axis=0, tiled=False)
    block = lax.axis_index(SEQ)
    intra_part = local_terms(queries, key_rows, values, cumulated, input_log)
    numerator = carried_terms(queries, cumulated, gathered, block) + intra_part
    row_mean = jnp.mean(numerator, axis=-1, keepdims=True)
    centred = numerator - row_mean
    row_var = jnp.mean(centred * centred, axis=-1, keepdims=True)
    normed = (centred * lax.rsqrt(row_var + 1e-05) * norm_gain).astype(jnp.bfloat16)
    head_terms = jnp.einsum(
        "vtr,edrc->vtedc", normed, columns_all.reshape(inner_size, outer, head_size, -1),
        preferred_element_type=jnp.float32,
    ).astype(jnp.bfloat16)
    head_terms = jnp.roll(head_terms, lax.axis_index(SEQ[1]) - inner_size // 2, axis=2)
    head_terms = jnp.roll(head_terms, lax.axis_index(SEQ[0]) - outer // 2, axis=3)
    head_terms = jnp.swapaxes(head_terms, 2, 3).reshape(*normed.shape[:2], -1)
    pair, across = HEAD
    blocks = head_terms.reshape(*head_terms.shape[:2], lax.axis_size(across), lax.axis_size(pair), -1)
    arrived = lax.all_to_all(blocks, pair, split_axis=3, concat_axis=3, tiled=True)
    pair_sum = jnp.sum(arrived.astype(jnp.float32), axis=3).astype(jnp.bfloat16)
    summed = lax.all_to_all(pair_sum, across, split_axis=2, concat_axis=2, tiled=True)
    summed = jnp.sum(summed.astype(jnp.float32), axis=2)
    return (residual_in[None, :, :].astype(jnp.float32) + summed).astype(jnp.bfloat16)


def solution(mesh):
    split = Mesh(
        mesh.devices.reshape(4, 8, mesh.shape["head"] // 2, 2, mesh.shape["var"]),
        ("seq_0", "seq_1", "head_0", "head_1", "var"),
    )
    heads = HEAD[::-1]
    placed = (
        P(SEQ, heads),
        P(SEQ, heads),
        P("var", SEQ),
        P(None, heads),
        P(heads, None, None),
        P(heads, None, None),
        P(heads, None),
        P(heads),
        P(heads, SEQ),
    )
    return jax.shard_map(
        body, mesh=split, in_specs=placed, out_specs=P("var", SEQ, heads), check_vma=False
    )
```

```python
import jax
import jax.numpy as jnp
from jax import lax
from jax.sharding import Mesh
from jax.sharding import PartitionSpec as P

CONV = 4
SEQ = ("seq_0", "seq_1")
HEAD = ("head_1", "head_0")
EXTRA = 8


def from_behind(value, axis, steps):
    count = lax.axis_size(axis)
    initial, last = (max(0, -steps), min(count, count - steps))
    return lax.ppermute(value, axis, [(source, source + steps) for source in range(initial, last)])


def split_up(x, dim, size):
    lengths = x.shape
    blocks = x.reshape(*lengths[:dim], size, lengths[dim] // size, *lengths[dim + 1 :])
    return jnp.moveaxis(blocks, dim, 0)


def sent_and_summed(x, axis, dim):
    blocks = split_up(x, dim, lax.axis_size(axis))
    arrived = lax.all_to_all(blocks, axis, split_axis=0, concat_axis=0, tiled=True)
    return arrived.astype(jnp.float32).sum(axis=0)


def ring_pieces(x, axis, count):
    ahead = [(i, (i + 1) % count) for i in range(count)]
    behind = [(i, (i - 1) % count) for i in range(count)]
    before, after = [], []
    forward = backward = x
    for k in range(1, count // 2 + 1):
        forward = lax.ppermute(forward, axis, ahead)
        before.append(forward)
        if k < count - k:
            backward = lax.ppermute(backward, axis, behind)
            after.append(backward)
    return jnp.stack(before[::-1] + [x] + after)


def three_parts(x):
    hi = lax.reduce_precision(x, exponent_bits=8, mantissa_bits=7)
    rest = x - hi
    mid = lax.reduce_precision(rest, exponent_bits=8, mantissa_bits=7)
    lo = rest - mid
    return jnp.stack([hi, mid, lo], axis=-1).astype(jnp.bfloat16)


def local_terms(queries, key_rows, values, cumulated, input_log):
    token_count = queries.shape[1]
    causal = jnp.arange(token_count)[:, None] >= jnp.arange(token_count)[None, :]
    scores = jnp.einsum("vtd,vsd->vts", queries, key_rows, preferred_element_type=jnp.float32)
    exponent = cumulated[:, :, None] - cumulated[:, None, :] + input_log[:, None, :]
    weights = (scores * jnp.exp(jnp.where(causal, exponent, -jnp.inf))).astype(jnp.bfloat16)
    return jnp.einsum("vts,vse->vte", weights, values, preferred_element_type=jnp.float32)


def carried_terms(queries, cumulated, gathered, block):
    blocks, rows, head_size = gathered.shape
    token_count = queries.shape[1]
    keys_all = gathered[:, :token_count, :].reshape(blocks * token_count, head_size)
    values_all = gathered[:, token_count : 2 * token_count, :].reshape(blocks * token_count, head_size)
    parts = gathered[:, 2 * token_count, :3].astype(jnp.float32)
    decay = (parts[:, 0] + parts[:, 1]) + parts[:, 2]
    through = jnp.cumsum(decay)
    before_own = jnp.sum(jnp.where(jnp.arange(blocks) < block, decay, 0.0))
    earlier = jnp.arange(blocks) < block
    block_exponent = jnp.where(earlier, before_own - through, -jnp.inf)
    scale = jnp.exp(cumulated[:, :, None] + block_exponent[None, None, :])
    scores = jnp.einsum("vtd,sd->vts", queries, keys_all, preferred_element_type=jnp.float32)
    scores = scores.reshape(*cumulated.shape, blocks, token_count) * scale[..., None]
    weights = scores.reshape(*cumulated.shape, blocks * token_count).astype(jnp.bfloat16)
    return jnp.einsum("vts,se->vte", weights, values_all, preferred_element_type=jnp.float32)


def body(
    inner,
    residual_in,
    erase,
    conv_weight,
    qkv_weight,
    gate_weight,
    gate_bias,
    norm_gain,
    down_weight,
):
    outer, inner_size = (lax.axis_size(SEQ[0]), lax.axis_size(SEQ[1]))
    columns_all = ring_pieces(ring_pieces(down_weight, SEQ[0], outer), SEQ[1], inner_size)
    kept_mask = (1 - erase).astype(jnp.bfloat16)
    erased = inner[None, :, :] * kept_mask[:, :, None]
    row_count = inner.shape[0]
    last_rows = erased[:, row_count - (CONV - 1) :, :]
    prior_rows = from_behind(last_rows, SEQ, 1)
    window = jnp.concatenate([prior_rows, erased], axis=1).astype(jnp.float32)
    convolved = jnp.zeros(erased.shape, jnp.float32)
    for offset in range(CONV):
        convolved = (
            convolved
            + conv_weight[offset] * window[:, CONV - 1 - offset : CONV - 1 - offset + row_count]
        )
    activated = jax.nn.silu(convolved).astype(jnp.bfloat16)
    proj_head = qkv_weight[0]
    head_size = proj_head.shape[0]
    query_key = jnp.einsum(
        "vtd,de->vte", activated, proj_head[:, : 2 * head_size], preferred_element_type=jnp.float32
    )
    queries = query_key[..., :head_size].astype(jnp.bfloat16)
    key_rows = (query_key[..., head_size:] * head_size ** (-0.5)).astype(jnp.bfloat16)
    values = jnp.einsum(
        "vtd,de->vte", erased, proj_head[:, 2 * head_size :], preferred_element_type=jnp.float32
    ).astype(jnp.bfloat16)
    gate_pre = (
        jnp.einsum("vtd,gd->vtg", activated, gate_weight[0], preferred_element_type=jnp.float32)
        + gate_bias[0]
    )
    input_log = 15.0 * jnp.tanh(gate_pre[..., 0] / 15.0)
    forget_log = jax.nn.log_sigmoid(gate_pre[..., 1])
    cumulated = jnp.cumsum(forget_log, axis=1)
    block_decay = cumulated[:, -1]
    key_scale = jnp.exp(block_decay[:, None] - cumulated + input_log)
    scaled_keys = (key_scale[..., None] * key_rows.astype(jnp.float32)).astype(jnp.bfloat16)
    extra = jnp.zeros((EXTRA, head_size), jnp.bfloat16)
    extra = extra.at[0, :3].set(three_parts(block_decay[0]))
    packed = jnp.concatenate([scaled_keys[0], values[0], extra], axis=0)
    gathered = lax.all_gather(packed, SEQ, axis=0, tiled=False)
    block = lax.axis_index(SEQ)
    intra_part = local_terms(queries, key_rows, values, cumulated, input_log)
    numerator = carried_terms(queries, cumulated, gathered, block) + intra_part
    row_mean = jnp.mean(numerator, axis=-1, keepdims=True)
    centred = numerator - row_mean
    row_var = jnp.mean(centred * centred, axis=-1, keepdims=True)
    normed = (centred * lax.rsqrt(row_var + 1e-05) * norm_gain).astype(jnp.bfloat16)
    head_terms = jnp.einsum(
        "vtr,edrc->vtedc", normed, columns_all.reshape(inner_size, outer, head_size, -1),
        preferred_element_type=jnp.float32,
    ).astype(jnp.bfloat16)
    head_terms = jnp.roll(head_terms, lax.axis_index(SEQ[1]) - inner_size // 2, axis=2)
    head_terms = jnp.roll(head_terms, lax.axis_index(SEQ[0]) - outer // 2, axis=3)
    head_terms = jnp.swapaxes(head_terms, 2, 3).reshape(*normed.shape[:2], -1)
    pair, across = HEAD
    blocks = head_terms.reshape(*head_terms.shape[:2], lax.axis_size(across), lax.axis_size(pair), -1)
    arrived = lax.all_to_all(blocks, pair, split_axis=3, concat_axis=3, tiled=True)
    pair_sum = jnp.sum(arrived.astype(jnp.float32), axis=3).astype(jnp.bfloat16)
    summed = lax.all_to_all(pair_sum, across, split_axis=2, concat_axis=2, tiled=True)
    summed = jnp.sum(summed.astype(jnp.float32), axis=2)
    return (residual_in[None, :, :].astype(jnp.float32) + summed).astype(jnp.bfloat16)


def solution(mesh):
    split = Mesh(
        mesh.devices.reshape(4, 8, mesh.shape["head"] // 2, 2, mesh.shape["var"]),
        ("seq_0", "seq_1", "head_0", "head_1", "var"),
    )
    heads = HEAD[::-1]
    placed = (
        P(SEQ, heads),
        P(SEQ, heads),
        P("var", SEQ),
        P(None, heads),
        P(heads, None, None),
        P(heads, None, None),
        P(heads, None),
        P(heads),
        P(heads, SEQ),
    )
    return jax.shard_map(
        body, mesh=split, in_specs=placed, out_specs=P("var", SEQ, heads), check_vma=False
    )
```

```python
import jax
import jax.numpy as jnp
from jax import lax
from jax.sharding import Mesh
from jax.sharding import PartitionSpec as P

CONV = 4
SEQ = ("seq_0", "seq_1")
HEAD = ("head_1", "head_0")
EXTRA = 8


def from_behind(value, axis, steps):
    count = lax.axis_size(axis)
    initial, last = (max(0, -steps), min(count, count - steps))
    return lax.ppermute(value, axis, [(source, source + steps) for source in range(initial, last)])


def split_up(x, dim, size):
    lengths = x.shape
    blocks = x.reshape(*lengths[:dim], size, lengths[dim] // size, *lengths[dim + 1 :])
    return jnp.moveaxis(blocks, dim, 0)


def sent_and_summed(x, axis, dim):
    blocks = split_up(x, dim, lax.axis_size(axis))
    arrived = lax.all_to_all(blocks, axis, split_axis=0, concat_axis=0, tiled=True)
    return arrived.astype(jnp.float32).sum(axis=0)


def ring_pieces(x, axis, count):
    ahead = [(i, (i + 1) % count) for i in range(count)]
    behind = [(i, (i - 1) % count) for i in range(count)]
    before, after = [], []
    forward = backward = x
    for k in range(1, count // 2 + 1):
        forward = lax.ppermute(forward, axis, ahead)
        before.append(forward)
        if k < count - k:
            backward = lax.ppermute(backward, axis, behind)
            after.append(backward)
    return jnp.stack(before[::-1] + [x] + after)


def three_parts(x):
    hi = lax.reduce_precision(x, exponent_bits=8, mantissa_bits=7)
    rest = x - hi
    mid = lax.reduce_precision(rest, exponent_bits=8, mantissa_bits=7)
    lo = rest - mid
    return jnp.stack([hi, mid, lo], axis=-1).astype(jnp.bfloat16)


def local_terms(queries, key_rows, values, cumulated, input_log):
    token_count = queries.shape[1]
    causal = jnp.arange(token_count)[:, None] >= jnp.arange(token_count)[None, :]
    scores = jnp.einsum("vtd,vsd->vts", queries, key_rows, preferred_element_type=jnp.float32)
    exponent = cumulated[:, :, None] - cumulated[:, None, :] + input_log[:, None, :]
    weights = (scores * jnp.exp(jnp.where(causal, exponent, -jnp.inf))).astype(jnp.bfloat16)
    return jnp.einsum("vts,vse->vte", weights, values, preferred_element_type=jnp.float32)


def carried_terms(queries, cumulated, gathered, block):
    blocks, rows, head_size = gathered.shape
    token_count = queries.shape[1]
    keys_all = gathered[:, :token_count, :].reshape(blocks * token_count, head_size)
    values_all = gathered[:, token_count : 2 * token_count, :].reshape(blocks * token_count, head_size)
    parts = gathered[:, 2 * token_count, :3].astype(jnp.float32)
    decay = (parts[:, 0] + parts[:, 1]) + parts[:, 2]
    through = jnp.cumsum(decay)
    before_own = jnp.sum(jnp.where(jnp.arange(blocks) < block, decay, 0.0))
    earlier = jnp.arange(blocks) < block
    block_exponent = jnp.where(earlier, before_own - through, -jnp.inf)
    scale = jnp.exp(cumulated[:, :, None] + block_exponent[None, None, :])
    scores = jnp.einsum("vtd,sd->vts", queries, keys_all, preferred_element_type=jnp.float32)
    scores = scores.reshape(*cumulated.shape, blocks, token_count) * scale[..., None]
    weights = scores.reshape(*cumulated.shape, blocks * token_count).astype(jnp.bfloat16)
    return jnp.einsum("vts,se->vte", weights, values_all, preferred_element_type=jnp.float32)


def body(
    inner,
    residual_in,
    erase,
    conv_weight,
    qkv_weight,
    gate_weight,
    gate_bias,
    norm_gain,
    down_weight,
):
    outer, inner_size = (lax.axis_size(SEQ[0]), lax.axis_size(SEQ[1]))
    columns_all = ring_pieces(ring_pieces(down_weight, SEQ[1], inner_size), SEQ[0], outer)
    kept_mask = (1 - erase).astype(jnp.bfloat16)
    erased = inner[None, :, :] * kept_mask[:, :, None]
    row_count = inner.shape[0]
    last_rows = erased[:, row_count - (CONV - 1) :, :]
    prior_rows = from_behind(last_rows, SEQ, 1)
    window = jnp.concatenate([prior_rows, erased], axis=1).astype(jnp.float32)
    convolved = jnp.zeros(erased.shape, jnp.float32)
    for offset in range(CONV):
        convolved = (
            convolved
            + conv_weight[offset] * window[:, CONV - 1 - offset : CONV - 1 - offset + row_count]
        )
    activated = jax.nn.silu(convolved).astype(jnp.bfloat16)
    proj_head = qkv_weight[0]
    head_size = proj_head.shape[0]
    query_key = jnp.einsum(
        "vtd,de->vte", activated, proj_head[:, : 2 * head_size], preferred_element_type=jnp.float32
    )
    queries = query_key[..., :head_size].astype(jnp.bfloat16)
    key_rows = (query_key[..., head_size:] * head_size ** (-0.5)).astype(jnp.bfloat16)
    values = jnp.einsum(
        "vtd,de->vte", erased, proj_head[:, 2 * head_size :], preferred_element_type=jnp.float32
    ).astype(jnp.bfloat16)
    gate_pre = (
        jnp.einsum("vtd,gd->vtg", activated, gate_weight[0], preferred_element_type=jnp.float32)
        + gate_bias[0]
    )
    input_log = 15.0 * jnp.tanh(gate_pre[..., 0] / 15.0)
    forget_log = jax.nn.log_sigmoid(gate_pre[..., 1])
    cumulated = jnp.cumsum(forget_log, axis=1)
    block_decay = cumulated[:, -1]
    key_scale = jnp.exp(block_decay[:, None] - cumulated + input_log)
    scaled_keys = (key_scale[..., None] * key_rows.astype(jnp.float32)).astype(jnp.bfloat16)
    extra = jnp.zeros((EXTRA, head_size), jnp.bfloat16)
    extra = extra.at[0, :3].set(three_parts(block_decay[0]))
    packed = jnp.concatenate([scaled_keys[0], values[0], extra], axis=0)
    gathered = lax.all_gather(packed, SEQ, axis=0, tiled=False)
    block = lax.axis_index(SEQ)
    intra_part = local_terms(queries, key_rows, values, cumulated, input_log)
    numerator = carried_terms(queries, cumulated, gathered, block) + intra_part
    row_mean = jnp.mean(numerator, axis=-1, keepdims=True)
    centred = numerator - row_mean
    row_var = jnp.mean(centred * centred, axis=-1, keepdims=True)
    normed = (centred * lax.rsqrt(row_var + 1e-05) * norm_gain).astype(jnp.bfloat16)
    head_terms = jnp.einsum(
        "vtr,derc->vtdec", normed, columns_all.reshape(outer, inner_size, head_size, -1),
        preferred_element_type=jnp.float32,
    ).astype(jnp.bfloat16)
    head_terms = jnp.roll(head_terms, lax.axis_index(SEQ[0]) - outer // 2, axis=2)
    head_terms = jnp.roll(head_terms, lax.axis_index(SEQ[1]) - inner_size // 2, axis=3)
    head_terms = head_terms.reshape(*normed.shape[:2], -1)
    pair, across = HEAD
    blocks = head_terms.reshape(*head_terms.shape[:2], lax.axis_size(across), lax.axis_size(pair), -1)
    arrived = lax.all_to_all(blocks, pair, split_axis=3, concat_axis=3, tiled=True)
    pair_sum = jnp.sum(arrived.astype(jnp.float32), axis=3).astype(jnp.bfloat16)
    summed = lax.all_to_all(pair_sum, across, split_axis=2, concat_axis=2, tiled=True)
    summed = jnp.sum(summed.astype(jnp.float32), axis=2)
    return (residual_in[None, :, :].astype(jnp.float32) + summed).astype(jnp.bfloat16)


def solution(mesh):
    split = Mesh(
        mesh.devices.reshape(4, 8, mesh.shape["head"] // 2, 2, mesh.shape["var"]),
        ("seq_0", "seq_1", "head_0", "head_1", "var"),
    )
    heads = HEAD[::-1]
    placed = (
        P(SEQ, heads),
        P(SEQ, heads),
        P("var", SEQ),
        P(None, heads),
        P(heads, None, None),
        P(heads, None, None),
        P(heads, None),
        P(heads),
        P(heads, SEQ),
    )
    return jax.shard_map(
        body, mesh=split, in_specs=placed, out_specs=P("var", SEQ, heads), check_vma=False
    )
```

```python
import jax
import jax.numpy as jnp
from jax import lax
from jax.sharding import Mesh
from jax.sharding import PartitionSpec as P

CONV = 4
SEQ = ("seq_0", "seq_1")
HEAD = ("head_1", "head_0")
EXTRA = 8


def from_behind(value, axis, steps):
    count = lax.axis_size(axis)
    initial, last = (max(0, -steps), min(count, count - steps))
    return lax.ppermute(value, axis, [(source, source + steps) for source in range(initial, last)])


def split_up(x, dim, size):
    lengths = x.shape
    blocks = x.reshape(*lengths[:dim], size, lengths[dim] // size, *lengths[dim + 1 :])
    return jnp.moveaxis(blocks, dim, 0)


def sent_and_summed(x, axis, dim):
    blocks = split_up(x, dim, lax.axis_size(axis))
    arrived = lax.all_to_all(blocks, axis, split_axis=0, concat_axis=0, tiled=True)
    return arrived.astype(jnp.float32).sum(axis=0)


def ring_pieces(x, axis, count):
    ahead = [(i, (i + 1) % count) for i in range(count)]
    behind = [(i, (i - 1) % count) for i in range(count)]
    before, after = [], []
    forward = backward = x
    for k in range(1, count // 2 + 1):
        forward = lax.ppermute(forward, axis, ahead)
        before.append(forward)
        if k < count - k:
            backward = lax.ppermute(backward, axis, behind)
            after.append(backward)
    return jnp.stack(before[::-1] + [x] + after)


def three_parts(x):
    hi = lax.reduce_precision(x, exponent_bits=8, mantissa_bits=7)
    rest = x - hi
    mid = lax.reduce_precision(rest, exponent_bits=8, mantissa_bits=7)
    lo = rest - mid
    return jnp.stack([hi, mid, lo], axis=-1).astype(jnp.bfloat16)


def local_terms(queries, key_rows, values, cumulated, input_log):
    token_count = queries.shape[1]
    causal = jnp.arange(token_count)[:, None] >= jnp.arange(token_count)[None, :]
    scores = jnp.einsum("vtd,vsd->vts", queries, key_rows, preferred_element_type=jnp.float32)
    exponent = cumulated[:, :, None] - cumulated[:, None, :] + input_log[:, None, :]
    weights = (scores * jnp.exp(jnp.where(causal, exponent, -jnp.inf))).astype(jnp.bfloat16)
    return jnp.einsum("vts,vse->vte", weights, values, preferred_element_type=jnp.float32)


def carried_terms(queries, cumulated, gathered, block):
    blocks, rows, head_size = gathered.shape
    token_count = queries.shape[1]
    keys_all = gathered[:, :token_count, :].reshape(blocks * token_count, head_size)
    values_all = gathered[:, token_count : 2 * token_count, :].reshape(blocks * token_count, head_size)
    parts = gathered[:, 2 * token_count, :3].astype(jnp.float32)
    decay = (parts[:, 0] + parts[:, 1]) + parts[:, 2]
    through = jnp.cumsum(decay)
    before_own = jnp.sum(jnp.where(jnp.arange(blocks) < block, decay, 0.0))
    earlier = jnp.arange(blocks) < block
    block_exponent = jnp.where(earlier, before_own - through, -jnp.inf)
    scale = jnp.exp(cumulated[:, :, None] + block_exponent[None, None, :])
    scores = jnp.einsum("vtd,sd->vts", queries, keys_all, preferred_element_type=jnp.float32)
    scores = scores.reshape(*cumulated.shape, blocks, token_count) * scale[..., None]
    weights = scores.reshape(*cumulated.shape, blocks * token_count).astype(jnp.bfloat16)
    return jnp.einsum("vts,se->vte", weights, values_all, preferred_element_type=jnp.float32)


def body(
    inner,
    residual_in,
    erase,
    conv_weight,
    qkv_weight,
    gate_weight,
    gate_bias,
    norm_gain,
    down_weight,
):
    outer, inner_size = (lax.axis_size(SEQ[0]), lax.axis_size(SEQ[1]))
    columns_all = ring_pieces(ring_pieces(down_weight, SEQ[0], outer), SEQ[1], inner_size)
    columns_all = jnp.roll(columns_all, lax.axis_index(SEQ[1]) - inner_size // 2, axis=0)
    columns_all = jnp.roll(columns_all, lax.axis_index(SEQ[0]) - outer // 2, axis=1)
    kept_mask = (1 - erase).astype(jnp.bfloat16)
    erased = inner[None, :, :] * kept_mask[:, :, None]
    row_count = inner.shape[0]
    last_rows = erased[:, row_count - (CONV - 1) :, :]
    prior_rows = from_behind(last_rows, SEQ, 1)
    window = jnp.concatenate([prior_rows, erased], axis=1).astype(jnp.float32)
    convolved = jnp.zeros(erased.shape, jnp.float32)
    for offset in range(CONV):
        convolved = (
            convolved
            + conv_weight[offset] * window[:, CONV - 1 - offset : CONV - 1 - offset + row_count]
        )
    activated = jax.nn.silu(convolved).astype(jnp.bfloat16)
    proj_head = qkv_weight[0]
    head_size = proj_head.shape[0]
    query_key = jnp.einsum(
        "vtd,de->vte", activated, proj_head[:, : 2 * head_size], preferred_element_type=jnp.float32
    )
    queries = query_key[..., :head_size].astype(jnp.bfloat16)
    key_rows = (query_key[..., head_size:] * head_size ** (-0.5)).astype(jnp.bfloat16)
    values = jnp.einsum(
        "vtd,de->vte", erased, proj_head[:, 2 * head_size :], preferred_element_type=jnp.float32
    ).astype(jnp.bfloat16)
    gate_pre = (
        jnp.einsum("vtd,gd->vtg", activated, gate_weight[0], preferred_element_type=jnp.float32)
        + gate_bias[0]
    )
    input_log = 15.0 * jnp.tanh(gate_pre[..., 0] / 15.0)
    forget_log = jax.nn.log_sigmoid(gate_pre[..., 1])
    cumulated = jnp.cumsum(forget_log, axis=1)
    block_decay = cumulated[:, -1]
    key_scale = jnp.exp(block_decay[:, None] - cumulated + input_log)
    scaled_keys = (key_scale[..., None] * key_rows.astype(jnp.float32)).astype(jnp.bfloat16)
    extra = jnp.zeros((EXTRA, head_size), jnp.bfloat16)
    extra = extra.at[0, :3].set(three_parts(block_decay[0]))
    packed = jnp.concatenate([scaled_keys[0], values[0], extra], axis=0)
    gathered = lax.all_gather(packed, SEQ, axis=0, tiled=False)
    block = lax.axis_index(SEQ)
    intra_part = local_terms(queries, key_rows, values, cumulated, input_log)
    numerator = carried_terms(queries, cumulated, gathered, block) + intra_part
    row_mean = jnp.mean(numerator, axis=-1, keepdims=True)
    centred = numerator - row_mean
    row_var = jnp.mean(centred * centred, axis=-1, keepdims=True)
    normed = (centred * lax.rsqrt(row_var + 1e-05) * norm_gain).astype(jnp.bfloat16)
    head_terms = jnp.einsum(
        "vtr,edrc->vtdec", normed, columns_all, preferred_element_type=jnp.float32
    ).astype(jnp.bfloat16)
    head_terms = head_terms.reshape(*normed.shape[:2], -1)
    pair, across = HEAD
    blocks = head_terms.reshape(*head_terms.shape[:2], lax.axis_size(across), lax.axis_size(pair), -1)
    arrived = lax.all_to_all(blocks, pair, split_axis=3, concat_axis=3, tiled=True)
    pair_sum = jnp.sum(arrived.astype(jnp.float32), axis=3).astype(jnp.bfloat16)
    summed = lax.all_to_all(pair_sum, across, split_axis=2, concat_axis=2, tiled=True)
    summed = jnp.sum(summed.astype(jnp.float32), axis=2)
    return (residual_in[None, :, :].astype(jnp.float32) + summed).astype(jnp.bfloat16)


def solution(mesh):
    split = Mesh(
        mesh.devices.reshape(4, 8, mesh.shape["head"] // 2, 2, mesh.shape["var"]),
        ("seq_0", "seq_1", "head_0", "head_1", "var"),
    )
    heads = HEAD[::-1]
    placed = (
        P(SEQ, heads),
        P(SEQ, heads),
        P("var", SEQ),
        P(None, heads),
        P(heads, None, None),
        P(heads, None, None),
        P(heads, None),
        P(heads),
        P(heads, SEQ),
    )
    return jax.shard_map(
        body, mesh=split, in_specs=placed, out_specs=P("var", SEQ, heads), check_vma=False
    )
```

```python
import jax
import jax.numpy as jnp
from jax import lax
from jax.sharding import Mesh
from jax.sharding import PartitionSpec as P

CONV = 4
SEQ = ("seq_0", "seq_1")
HEAD = ("head_1", "head_0")
EXTRA = 8


def from_behind(value, axis, steps):
    count = lax.axis_size(axis)
    initial, last = (max(0, -steps), min(count, count - steps))
    return lax.ppermute(value, axis, [(source, source + steps) for source in range(initial, last)])


def split_up(x, dim, size):
    lengths = x.shape
    blocks = x.reshape(*lengths[:dim], size, lengths[dim] // size, *lengths[dim + 1 :])
    return jnp.moveaxis(blocks, dim, 0)


def sent_and_summed(x, axis, dim):
    blocks = split_up(x, dim, lax.axis_size(axis))
    arrived = lax.all_to_all(blocks, axis, split_axis=0, concat_axis=0, tiled=True)
    return arrived.astype(jnp.float32).sum(axis=0)


def ring_pieces(x, axis, count):
    ahead = [(i, (i + 1) % count) for i in range(count)]
    behind = [(i, (i - 1) % count) for i in range(count)]
    before, after = [], []
    forward = backward = x
    for k in range(1, count // 2 + 1):
        forward = lax.ppermute(forward, axis, ahead)
        before.append(forward)
        if k < count - k:
            backward = lax.ppermute(backward, axis, behind)
            after.append(backward)
    return jnp.stack(before[::-1] + [x] + after)


def three_parts(x):
    hi = lax.reduce_precision(x, exponent_bits=8, mantissa_bits=7)
    rest = x - hi
    mid = lax.reduce_precision(rest, exponent_bits=8, mantissa_bits=7)
    lo = rest - mid
    return jnp.stack([hi, mid, lo], axis=-1).astype(jnp.bfloat16)


def local_terms(queries, key_rows, values, cumulated, input_log):
    token_count = queries.shape[1]
    causal = jnp.arange(token_count)[:, None] >= jnp.arange(token_count)[None, :]
    scores = jnp.einsum("vtd,vsd->vts", queries, key_rows, preferred_element_type=jnp.float32)
    exponent = cumulated[:, :, None] - cumulated[:, None, :] + input_log[:, None, :]
    weights = (scores * jnp.exp(jnp.where(causal, exponent, -jnp.inf))).astype(jnp.bfloat16)
    return jnp.einsum("vts,vse->vte", weights, values, preferred_element_type=jnp.float32)


def carried_terms(queries, cumulated, gathered, block):
    blocks, rows, head_size = gathered.shape
    token_count = queries.shape[1]
    keys_all = gathered[:, :token_count, :].reshape(blocks * token_count, head_size)
    values_all = gathered[:, token_count : 2 * token_count, :].reshape(blocks * token_count, head_size)
    parts = gathered[:, 2 * token_count, :3].astype(jnp.float32)
    decay = (parts[:, 0] + parts[:, 1]) + parts[:, 2]
    index = jnp.arange(blocks)
    between = (index[:, None] < index[None, :]) & (index[None, :] < block)
    before_own = jnp.sum(jnp.where(index < block, decay, 0.0))
    block_exponent = jnp.where(index < block, jnp.sum(jnp.where(between, decay[None, :], 0.0), axis=1), -jnp.inf)
    scale = jnp.exp(cumulated[:, :, None] + block_exponent[None, None, :])
    scores = jnp.einsum("vtd,sd->vts", queries, keys_all, preferred_element_type=jnp.float32)
    scores = scores.reshape(*cumulated.shape, blocks, token_count) * scale[..., None]
    weights = scores.reshape(*cumulated.shape, blocks * token_count).astype(jnp.bfloat16)
    return jnp.einsum("vts,se->vte", weights, values_all, preferred_element_type=jnp.float32)


def body(
    inner,
    residual_in,
    erase,
    conv_weight,
    qkv_weight,
    gate_weight,
    gate_bias,
    norm_gain,
    down_weight,
):
    outer, inner_size = (lax.axis_size(SEQ[0]), lax.axis_size(SEQ[1]))
    columns_all = ring_pieces(ring_pieces(down_weight, SEQ[0], outer), SEQ[1], inner_size)
    kept_mask = (1 - erase).astype(jnp.bfloat16)
    erased = inner[None, :, :] * kept_mask[:, :, None]
    row_count = inner.shape[0]
    last_rows = erased[:, row_count - (CONV - 1) :, :]
    prior_rows = from_behind(last_rows, SEQ, 1)
    window = jnp.concatenate([prior_rows, erased], axis=1).astype(jnp.float32)
    convolved = jnp.zeros(erased.shape, jnp.float32)
    for offset in range(CONV):
        convolved = (
            convolved
            + conv_weight[offset] * window[:, CONV - 1 - offset : CONV - 1 - offset + row_count]
        )
    activated = jax.nn.silu(convolved).astype(jnp.bfloat16)
    proj_head = qkv_weight[0]
    head_size = proj_head.shape[0]
    query_key = jnp.einsum(
        "vtd,de->vte", activated, proj_head[:, : 2 * head_size], preferred_element_type=jnp.float32
    )
    queries = query_key[..., :head_size].astype(jnp.bfloat16)
    key_rows = (query_key[..., head_size:] * head_size ** (-0.5)).astype(jnp.bfloat16)
    values = jnp.einsum(
        "vtd,de->vte", erased, proj_head[:, 2 * head_size :], preferred_element_type=jnp.float32
    ).astype(jnp.bfloat16)
    gate_pre = (
        jnp.einsum("vtd,gd->vtg", activated, gate_weight[0], preferred_element_type=jnp.float32)
        + gate_bias[0]
    )
    input_log = 15.0 * jnp.tanh(gate_pre[..., 0] / 15.0)
    forget_log = jax.nn.log_sigmoid(gate_pre[..., 1])
    cumulated = jnp.cumsum(forget_log, axis=1)
    block_decay = cumulated[:, -1]
    key_scale = jnp.exp(block_decay[:, None] - cumulated + input_log)
    scaled_keys = (key_scale[..., None] * key_rows.astype(jnp.float32)).astype(jnp.bfloat16)
    extra = jnp.zeros((EXTRA, head_size), jnp.bfloat16)
    extra = extra.at[0, :3].set(three_parts(block_decay[0]))
    packed = jnp.concatenate([scaled_keys[0], values[0], extra], axis=0)
    gathered = lax.all_gather(packed, SEQ, axis=0, tiled=False)
    block = lax.axis_index(SEQ)
    intra_part = local_terms(queries, key_rows, values, cumulated, input_log)
    numerator = carried_terms(queries, cumulated, gathered, block) + intra_part
    row_mean = jnp.mean(numerator, axis=-1, keepdims=True)
    centred = numerator - row_mean
    row_var = jnp.mean(centred * centred, axis=-1, keepdims=True)
    normed = (centred * lax.rsqrt(row_var + 1e-05) * norm_gain).astype(jnp.bfloat16)
    head_terms = jnp.einsum(
        "vtr,edrc->vtedc", normed, columns_all.reshape(inner_size, outer, head_size, -1),
        preferred_element_type=jnp.float32,
    ).astype(jnp.bfloat16)
    head_terms = jnp.roll(head_terms, lax.axis_index(SEQ[1]) - inner_size // 2, axis=2)
    head_terms = jnp.roll(head_terms, lax.axis_index(SEQ[0]) - outer // 2, axis=3)
    head_terms = jnp.swapaxes(head_terms, 2, 3).reshape(*normed.shape[:2], -1)
    pair, across = HEAD
    blocks = head_terms.reshape(*head_terms.shape[:2], lax.axis_size(across), lax.axis_size(pair), -1)
    arrived = lax.all_to_all(blocks, pair, split_axis=3, concat_axis=3, tiled=True)
    pair_sum = jnp.sum(arrived.astype(jnp.float32), axis=3).astype(jnp.bfloat16)
    summed = lax.all_to_all(pair_sum, across, split_axis=2, concat_axis=2, tiled=True)
    summed = jnp.sum(summed.astype(jnp.float32), axis=2)
    return (residual_in[None, :, :].astype(jnp.float32) + summed).astype(jnp.bfloat16)


def solution(mesh):
    split = Mesh(
        mesh.devices.reshape(4, 8, mesh.shape["head"] // 2, 2, mesh.shape["var"]),
        ("seq_0", "seq_1", "head_0", "head_1", "var"),
    )
    heads = HEAD[::-1]
    placed = (
        P(SEQ, heads),
        P(SEQ, heads),
        P("var", SEQ),
        P(None, heads),
        P(heads, None, None),
        P(heads, None, None),
        P(heads, None),
        P(heads),
        P(heads, SEQ),
    )
    return jax.shard_map(
        body, mesh=split, in_specs=placed, out_specs=P("var", SEQ, heads), check_vma=False
    )
```

```python
import jax
import jax.numpy as jnp
from jax import lax
from jax.sharding import Mesh
from jax.sharding import PartitionSpec as P

CONV = 4
SEQ = ("seq_0", "seq_1")
HEAD = ("head_1", "head_0")
EXTRA = 8


def from_behind(value, axis, steps):
    count = lax.axis_size(axis)
    initial, last = (max(0, -steps), min(count, count - steps))
    return lax.ppermute(value, axis, [(source, source + steps) for source in range(initial, last)])


def split_up(x, dim, size):
    lengths = x.shape
    blocks = x.reshape(*lengths[:dim], size, lengths[dim] // size, *lengths[dim + 1 :])
    return jnp.moveaxis(blocks, dim, 0)


def sent_and_summed(x, axis, dim):
    blocks = split_up(x, dim, lax.axis_size(axis))
    arrived = lax.all_to_all(blocks, axis, split_axis=0, concat_axis=0, tiled=True)
    return arrived.astype(jnp.float32).sum(axis=0)


def ring_pieces(x, axis, count):
    ahead = [(i, (i + 1) % count) for i in range(count)]
    behind = [(i, (i - 1) % count) for i in range(count)]
    before, after = [], []
    forward = backward = x
    for k in range(1, count // 2 + 1):
        forward = lax.ppermute(forward, axis, ahead)
        before.append(forward)
        if k < count - k:
            backward = lax.ppermute(backward, axis, behind)
            after.append(backward)
    return jnp.stack(before[::-1] + [x] + after)


def three_parts(x):
    hi = lax.reduce_precision(x, exponent_bits=8, mantissa_bits=7)
    rest = x - hi
    mid = lax.reduce_precision(rest, exponent_bits=8, mantissa_bits=7)
    lo = rest - mid
    return jnp.stack([hi, mid, lo], axis=-1).astype(jnp.bfloat16)


def local_terms(queries, key_rows, values, cumulated, input_log):
    token_count = queries.shape[1]
    causal = jnp.arange(token_count)[:, None] >= jnp.arange(token_count)[None, :]
    scores = jnp.einsum("vtd,vsd->vts", queries, key_rows, preferred_element_type=jnp.float32)
    exponent = cumulated[:, :, None] - cumulated[:, None, :] + input_log[:, None, :]
    weights = (scores * jnp.exp(jnp.where(causal, exponent, -jnp.inf))).astype(jnp.bfloat16)
    return jnp.einsum("vts,vse->vte", weights, values, preferred_element_type=jnp.float32)


def carried_terms(queries, cumulated, gathered, block):
    blocks, rows, head_size = gathered.shape
    token_count = queries.shape[1]
    keys_all = gathered[:, :token_count, :].reshape(blocks * token_count, head_size)
    values_all = gathered[:, token_count : 2 * token_count, :].reshape(blocks * token_count, head_size)
    parts = gathered[:, 2 * token_count, :3].astype(jnp.float32)
    decay = (parts[:, 0] + parts[:, 1]) + parts[:, 2]
    index = jnp.arange(blocks)
    between = (index[:, None] < index[None, :]) & (index[None, :] < block)
    before_own = jnp.sum(jnp.where(index < block, decay, 0.0))
    block_exponent = jnp.where(index < block, jnp.sum(jnp.where(between, decay[None, :], 0.0), axis=1), -jnp.inf)
    scale = jnp.exp(cumulated[:, :, None] + block_exponent[None, None, :])
    scores = jnp.einsum("vtd,sd->vts", queries, keys_all, preferred_element_type=jnp.float32)
    scores = scores.reshape(*cumulated.shape, blocks, token_count) * scale[..., None]
    weights = scores.reshape(*cumulated.shape, blocks * token_count).astype(jnp.bfloat16)
    return jnp.einsum("vts,se->vte", weights, values_all, preferred_element_type=jnp.float32)


def body(
    inner,
    residual_in,
    erase,
    conv_weight,
    qkv_weight,
    gate_weight,
    gate_bias,
    norm_gain,
    down_weight,
):
    outer, inner_size = (lax.axis_size(SEQ[0]), lax.axis_size(SEQ[1]))
    columns_all = ring_pieces(ring_pieces(down_weight, SEQ[0], outer), SEQ[1], inner_size)
    kept_mask = (1 - erase).astype(jnp.bfloat16)
    erased = inner[None, :, :] * kept_mask[:, :, None]
    row_count = inner.shape[0]
    last_rows = erased[:, row_count - (CONV - 1) :, :]
    prior_rows = from_behind(last_rows, SEQ, 1)
    window = jnp.concatenate([prior_rows, erased], axis=1).astype(jnp.float32)
    convolved = jnp.zeros(erased.shape, jnp.float32)
    for offset in range(CONV):
        convolved = (
            convolved
            + conv_weight[offset] * window[:, CONV - 1 - offset : CONV - 1 - offset + row_count]
        )
    activated = jax.nn.silu(convolved).astype(jnp.bfloat16)
    proj_head = qkv_weight[0]
    head_size = proj_head.shape[0]
    query_key = jnp.einsum(
        "vtd,de->vte", activated, proj_head[:, : 2 * head_size], preferred_element_type=jnp.float32
    )
    queries = query_key[..., :head_size].astype(jnp.bfloat16)
    key_rows = (query_key[..., head_size:] * head_size ** (-0.5)).astype(jnp.bfloat16)
    values = jnp.einsum(
        "vtd,de->vte", erased, proj_head[:, 2 * head_size :], preferred_element_type=jnp.float32
    ).astype(jnp.bfloat16)
    gate_pre = (
        jnp.einsum("vtd,gd->vtg", activated, gate_weight[0], preferred_element_type=jnp.float32)
        + gate_bias[0]
    )
    input_log = 15.0 * jnp.tanh(gate_pre[..., 0] / 15.0)
    forget_log = jax.nn.log_sigmoid(gate_pre[..., 1])
    cumulated = jnp.cumsum(forget_log, axis=1)
    block_decay = cumulated[:, -1]
    key_scale = jnp.exp(block_decay[:, None] - cumulated + input_log)
    scaled_keys = (key_scale[..., None] * key_rows.astype(jnp.float32)).astype(jnp.bfloat16)
    extra = jnp.zeros((EXTRA, head_size), jnp.bfloat16)
    extra = extra.at[0, :3].set(three_parts(block_decay[0]))
    packed = jnp.concatenate([scaled_keys[0], values[0], extra], axis=0)
    gathered = lax.all_gather(packed, SEQ, axis=0, tiled=False)
    block = lax.axis_index(SEQ)
    intra_part = local_terms(queries, key_rows, values, cumulated, input_log)
    numerator = carried_terms(queries, cumulated, gathered, block) + intra_part
    row_mean = jnp.mean(numerator, axis=-1, keepdims=True)
    centred = numerator - row_mean
    row_var = jnp.mean(centred * centred, axis=-1, keepdims=True)
    normed = (centred * lax.rsqrt(row_var + 1e-05) * norm_gain).astype(jnp.bfloat16)
    head_terms = jnp.einsum(
        "vtr,edrc->vtedc", normed, columns_all.reshape(inner_size, outer, head_size, -1),
        preferred_element_type=jnp.float32,
    ).astype(jnp.bfloat16)
    head_terms = jnp.roll(head_terms, lax.axis_index(SEQ[1]) - inner_size // 2, axis=2)
    head_terms = jnp.roll(head_terms, lax.axis_index(SEQ[0]) - outer // 2, axis=3)
    pair, across = HEAD
    pairs = lax.axis_size(pair)
    head_terms = head_terms.reshape(*normed.shape[:2], pairs, inner_size // pairs, outer, -1)
    blocks = jnp.transpose(head_terms, (2, 4, 0, 1, 3, 5)).reshape(pairs, outer, *normed.shape[:2], -1)
    arrived = lax.all_to_all(blocks, pair, split_axis=0, concat_axis=0, tiled=True)
    pair_sum = jnp.sum(arrived.astype(jnp.float32), axis=0).astype(jnp.bfloat16)
    summed = lax.all_to_all(pair_sum, across, split_axis=0, concat_axis=0, tiled=True)
    summed = jnp.sum(summed.astype(jnp.float32), axis=0)
    return (residual_in[None, :, :].astype(jnp.float32) + summed).astype(jnp.bfloat16)


def solution(mesh):
    split = Mesh(
        mesh.devices.reshape(4, 8, mesh.shape["head"] // 2, 2, mesh.shape["var"]),
        ("seq_0", "seq_1", "head_0", "head_1", "var"),
    )
    heads = HEAD[::-1]
    placed = (
        P(SEQ, heads),
        P(SEQ, heads),
        P("var", SEQ),
        P(None, heads),
        P(heads, None, None),
        P(heads, None, None),
        P(heads, None),
        P(heads),
        P(heads, SEQ),
    )
    return jax.shard_map(
        body, mesh=split, in_specs=placed, out_specs=P("var", SEQ, heads), check_vma=False
    )
```

```python
import jax
import jax.numpy as jnp
from jax import lax
from jax.sharding import Mesh
from jax.sharding import PartitionSpec as P

CONV = 4
SEQ = ("seq_0", "seq_1")
HEAD = ("head_1", "head_0")
EXTRA = 8


def from_behind(value, axis, steps):
    count = lax.axis_size(axis)
    initial, last = (max(0, -steps), min(count, count - steps))
    return lax.ppermute(value, axis, [(source, source + steps) for source in range(initial, last)])


def split_up(x, dim, size):
    lengths = x.shape
    blocks = x.reshape(*lengths[:dim], size, lengths[dim] // size, *lengths[dim + 1 :])
    return jnp.moveaxis(blocks, dim, 0)


def sent_and_summed(x, axis, dim):
    blocks = split_up(x, dim, lax.axis_size(axis))
    arrived = lax.all_to_all(blocks, axis, split_axis=0, concat_axis=0, tiled=True)
    return arrived.astype(jnp.float32).sum(axis=0)


def ring_pieces(x, axis, count):
    ahead = [(i, (i + 1) % count) for i in range(count)]
    behind = [(i, (i - 1) % count) for i in range(count)]
    before, after = [], []
    forward = backward = x
    for k in range(1, count // 2 + 1):
        forward = lax.ppermute(forward, axis, ahead)
        before.append(forward)
        if k < count - k:
            backward = lax.ppermute(backward, axis, behind)
            after.append(backward)
    return jnp.stack(before[::-1] + [x] + after)


def three_parts(x):
    hi = lax.reduce_precision(x, exponent_bits=8, mantissa_bits=7)
    rest = x - hi
    mid = lax.reduce_precision(rest, exponent_bits=8, mantissa_bits=7)
    lo = rest - mid
    return jnp.stack([hi, mid, lo], axis=-1).astype(jnp.bfloat16)


def local_terms(queries, key_rows, values, cumulated, input_log):
    token_count = queries.shape[1]
    causal = jnp.arange(token_count)[:, None] >= jnp.arange(token_count)[None, :]
    scores = jnp.einsum("vtd,vsd->vts", queries, key_rows, preferred_element_type=jnp.float32)
    exponent = cumulated[:, :, None] - cumulated[:, None, :] + input_log[:, None, :]
    weights = (scores * jnp.exp(jnp.where(causal, exponent, -jnp.inf))).astype(jnp.bfloat16)
    return jnp.einsum("vts,vse->vte", weights, values, preferred_element_type=jnp.float32)


def carried_terms(queries, cumulated, gathered, block):
    blocks, rows, head_size = gathered.shape
    token_count = queries.shape[1]
    keys_all = gathered[:, :token_count, :].reshape(blocks * token_count, head_size)
    values_all = gathered[:, token_count : 2 * token_count, :].reshape(blocks * token_count, head_size)
    parts = gathered[:, 2 * token_count, :].astype(jnp.float32)
    decay = jnp.sum(jnp.where(jnp.arange(head_size) < 3, parts, 0.0), axis=1)
    index = jnp.arange(blocks)
    between = (index[:, None] < index[None, :]) & (index[None, :] < block)
    before_own = jnp.sum(jnp.where(index < block, decay, 0.0))
    block_exponent = jnp.where(index < block, jnp.sum(jnp.where(between, decay[None, :], 0.0), axis=1), -jnp.inf)
    scale = jnp.exp(cumulated[:, :, None] + block_exponent[None, None, :])
    scores = jnp.einsum("vtd,sd->vts", queries, keys_all, preferred_element_type=jnp.float32)
    scores = scores.reshape(*cumulated.shape, blocks, token_count) * scale[..., None]
    weights = scores.reshape(*cumulated.shape, blocks * token_count).astype(jnp.bfloat16)
    return jnp.einsum("vts,se->vte", weights, values_all, preferred_element_type=jnp.float32)


def body(
    inner,
    residual_in,
    erase,
    conv_weight,
    qkv_weight,
    gate_weight,
    gate_bias,
    norm_gain,
    down_weight,
):
    outer, inner_size = (lax.axis_size(SEQ[0]), lax.axis_size(SEQ[1]))
    columns_all = ring_pieces(ring_pieces(down_weight, SEQ[0], outer), SEQ[1], inner_size)
    kept_mask = (1 - erase).astype(jnp.bfloat16)
    erased = inner[None, :, :] * kept_mask[:, :, None]
    row_count = inner.shape[0]
    last_rows = erased[:, row_count - (CONV - 1) :, :]
    prior_rows = from_behind(last_rows, SEQ, 1)
    window = jnp.concatenate([prior_rows, erased], axis=1).astype(jnp.float32)
    convolved = jnp.zeros(erased.shape, jnp.float32)
    for offset in range(CONV):
        convolved = (
            convolved
            + conv_weight[offset] * window[:, CONV - 1 - offset : CONV - 1 - offset + row_count]
        )
    activated = jax.nn.silu(convolved).astype(jnp.bfloat16)
    proj_head = qkv_weight[0]
    head_size = proj_head.shape[0]
    query_key = jnp.einsum(
        "vtd,de->vte", activated, proj_head[:, : 2 * head_size], preferred_element_type=jnp.float32
    )
    queries = query_key[..., :head_size].astype(jnp.bfloat16)
    key_rows = (query_key[..., head_size:] * head_size ** (-0.5)).astype(jnp.bfloat16)
    values = jnp.einsum(
        "vtd,de->vte", erased, proj_head[:, 2 * head_size :], preferred_element_type=jnp.float32
    ).astype(jnp.bfloat16)
    gate_pre = (
        jnp.einsum("vtd,gd->vtg", activated, gate_weight[0], preferred_element_type=jnp.float32)
        + gate_bias[0]
    )
    input_log = 15.0 * jnp.tanh(gate_pre[..., 0] / 15.0)
    forget_log = jax.nn.log_sigmoid(gate_pre[..., 1])
    cumulated = jnp.cumsum(forget_log, axis=1)
    block_decay = cumulated[:, -1]
    key_scale = jnp.exp(block_decay[:, None] - cumulated + input_log)
    scaled_keys = (key_scale[..., None] * key_rows.astype(jnp.float32)).astype(jnp.bfloat16)
    extra = jnp.zeros((EXTRA, head_size), jnp.bfloat16)
    extra = extra.at[0, :3].set(three_parts(block_decay[0]))
    packed = jnp.concatenate([scaled_keys[0], values[0], extra], axis=0)
    gathered = lax.all_gather(packed, SEQ, axis=0, tiled=False)
    block = lax.axis_index(SEQ)
    intra_part = local_terms(queries, key_rows, values, cumulated, input_log)
    numerator = carried_terms(queries, cumulated, gathered, block) + intra_part
    row_mean = jnp.mean(numerator, axis=-1, keepdims=True)
    centred = numerator - row_mean
    row_var = jnp.mean(centred * centred, axis=-1, keepdims=True)
    normed = (centred * lax.rsqrt(row_var + 1e-05) * norm_gain).astype(jnp.bfloat16)
    head_terms = jnp.einsum(
        "vtr,edrc->vtedc", normed, columns_all.reshape(inner_size, outer, head_size, -1),
        preferred_element_type=jnp.float32,
    ).astype(jnp.bfloat16)
    head_terms = jnp.roll(head_terms, lax.axis_index(SEQ[1]) - inner_size // 2, axis=2)
    head_terms = jnp.roll(head_terms, lax.axis_index(SEQ[0]) - outer // 2, axis=3)
    pair, across = HEAD
    pairs = lax.axis_size(pair)
    head_terms = head_terms.reshape(*normed.shape[:2], pairs, inner_size // pairs, outer, -1)
    blocks = jnp.transpose(head_terms, (2, 4, 0, 1, 3, 5)).reshape(pairs, outer, *normed.shape[:2], -1)
    arrived = lax.all_to_all(blocks, pair, split_axis=0, concat_axis=0, tiled=True)
    pair_sum = jnp.sum(arrived.astype(jnp.float32), axis=0).astype(jnp.bfloat16)
    summed = lax.all_to_all(pair_sum, across, split_axis=0, concat_axis=0, tiled=True)
    summed = jnp.sum(summed.astype(jnp.float32), axis=0)
    return (residual_in[None, :, :].astype(jnp.float32) + summed).astype(jnp.bfloat16)


def solution(mesh):
    split = Mesh(
        mesh.devices.reshape(4, 8, mesh.shape["head"] // 2, 2, mesh.shape["var"]),
        ("seq_0", "seq_1", "head_0", "head_1", "var"),
    )
    heads = HEAD[::-1]
    placed = (
        P(SEQ, heads),
        P(SEQ, heads),
        P("var", SEQ),
        P(None, heads),
        P(heads, None, None),
        P(heads, None, None),
        P(heads, None),
        P(heads),
        P(heads, SEQ),
    )
    return jax.shard_map(
        body, mesh=split, in_specs=placed, out_specs=P("var", SEQ, heads), check_vma=False
    )
```

```python
import jax
import jax.numpy as jnp
from jax import lax
from jax.sharding import Mesh
from jax.sharding import PartitionSpec as P

CONV = 4
SEQ = ("seq_0", "seq_1")
HEAD = ("head_1", "head_0")
EXTRA = 8


def from_behind(value, axis, steps):
    count = lax.axis_size(axis)
    initial, last = (max(0, -steps), min(count, count - steps))
    return lax.ppermute(value, axis, [(source, source + steps) for source in range(initial, last)])


def split_up(x, dim, size):
    lengths = x.shape
    blocks = x.reshape(*lengths[:dim], size, lengths[dim] // size, *lengths[dim + 1 :])
    return jnp.moveaxis(blocks, dim, 0)


def sent_and_summed(x, axis, dim):
    blocks = split_up(x, dim, lax.axis_size(axis))
    arrived = lax.all_to_all(blocks, axis, split_axis=0, concat_axis=0, tiled=True)
    return arrived.astype(jnp.float32).sum(axis=0)


def ring_pieces(x, axis, count):
    ahead = [(i, (i + 1) % count) for i in range(count)]
    behind = [(i, (i - 1) % count) for i in range(count)]
    before, after = [], []
    forward = backward = x
    for k in range(1, count // 2 + 1):
        forward = lax.ppermute(forward, axis, ahead)
        before.append(forward)
        if k < count - k:
            backward = lax.ppermute(backward, axis, behind)
            after.append(backward)
    return jnp.stack(before[::-1] + [x] + after)


def three_parts(x):
    hi = lax.reduce_precision(x, exponent_bits=8, mantissa_bits=7)
    rest = x - hi
    mid = lax.reduce_precision(rest, exponent_bits=8, mantissa_bits=7)
    lo = rest - mid
    return jnp.stack([hi, mid, lo], axis=-1).astype(jnp.bfloat16)


def local_terms(queries, key_rows, values, cumulated, input_log):
    token_count = queries.shape[1]
    causal = jnp.arange(token_count)[:, None] >= jnp.arange(token_count)[None, :]
    scores = jnp.einsum("vtd,vsd->vts", queries, key_rows, preferred_element_type=jnp.float32)
    exponent = cumulated[:, :, None] - cumulated[:, None, :] + input_log[:, None, :]
    weights = (scores * jnp.exp(jnp.where(causal, exponent, -jnp.inf))).astype(jnp.bfloat16)
    return jnp.einsum("vts,vse->vte", weights, values, preferred_element_type=jnp.float32)


def carried_terms(queries, cumulated, gathered, block):
    blocks, rows, head_size = gathered.shape
    token_count = queries.shape[1]
    keys_all = gathered[:, :token_count, :].reshape(blocks * token_count, head_size)
    values_all = gathered[:, token_count : 2 * token_count, :].reshape(blocks * token_count, head_size)
    parts = gathered[:, 2 * token_count, :].astype(jnp.float32)
    decay = jnp.sum(jnp.where(jnp.arange(head_size) < 3, parts, 0.0), axis=1)
    index = jnp.arange(blocks)
    between = (index[:, None] < index[None, :]) & (index[None, :] < block)
    before_own = jnp.sum(jnp.where(index < block, decay, 0.0))
    block_exponent = jnp.where(index < block, jnp.sum(jnp.where(between, decay[None, :], 0.0), axis=1), -jnp.inf)
    scale = jnp.exp(cumulated[:, :, None] + block_exponent[None, None, :])
    scores = jnp.einsum("vtd,sd->vts", queries, keys_all, preferred_element_type=jnp.float32)
    scores = scores.reshape(*cumulated.shape, blocks, token_count) * scale[..., None]
    weights = scores.reshape(*cumulated.shape, blocks * token_count).astype(jnp.bfloat16)
    return jnp.einsum("vts,se->vte", weights, values_all, preferred_element_type=jnp.float32)


def body(
    inner,
    residual_in,
    erase,
    conv_weight,
    qkv_weight,
    gate_weight,
    gate_bias,
    norm_gain,
    down_weight,
):
    outer, inner_size = (lax.axis_size(SEQ[0]), lax.axis_size(SEQ[1]))
    columns_all = ring_pieces(ring_pieces(down_weight, SEQ[0], outer), SEQ[1], inner_size)
    kept_mask = (1 - erase).astype(jnp.bfloat16)
    erased = inner[None, :, :] * kept_mask[:, :, None]
    row_count = inner.shape[0]
    last_rows = erased[:, row_count - (CONV - 1) :, :]
    prior_rows = from_behind(last_rows, SEQ, 1)
    window = jnp.concatenate([prior_rows, erased], axis=1).astype(jnp.float32)
    convolved = jnp.zeros(erased.shape, jnp.float32)
    for offset in range(CONV):
        convolved = (
            convolved
            + conv_weight[offset] * window[:, CONV - 1 - offset : CONV - 1 - offset + row_count]
        )
    activated = jax.nn.silu(convolved).astype(jnp.bfloat16)
    proj_head = qkv_weight[0]
    head_size = proj_head.shape[0]
    query_key = jnp.einsum(
        "vtd,de->vte", activated, proj_head[:, : 2 * head_size], preferred_element_type=jnp.float32
    )
    queries = query_key[..., :head_size].astype(jnp.bfloat16)
    key_rows = (query_key[..., head_size:] * head_size ** (-0.5)).astype(jnp.bfloat16)
    values = jnp.einsum(
        "vtd,de->vte", erased, proj_head[:, 2 * head_size :], preferred_element_type=jnp.float32
    ).astype(jnp.bfloat16)
    gate_pre = (
        jnp.einsum("vtd,gd->vtg", activated, gate_weight[0], preferred_element_type=jnp.float32)
        + gate_bias[0]
    )
    input_log = 15.0 * jnp.tanh(gate_pre[..., 0] / 15.0)
    forget_log = jax.nn.log_sigmoid(gate_pre[..., 1])
    cumulated = jnp.cumsum(forget_log, axis=1)
    block_decay = cumulated[:, -1]
    key_scale = jnp.exp(block_decay[:, None] - cumulated + input_log)
    scaled_keys = (key_scale[..., None] * key_rows.astype(jnp.float32)).astype(jnp.bfloat16)
    extra = jnp.zeros((EXTRA, head_size), jnp.bfloat16)
    extra = extra.at[0, :3].set(three_parts(block_decay[0]))
    packed = jnp.concatenate([scaled_keys[0], values[0], extra], axis=0)
    gathered = lax.all_gather(packed, SEQ, axis=0, tiled=False)
    block = lax.axis_index(SEQ)
    intra_part = local_terms(queries, key_rows, values, cumulated, input_log)
    numerator = carried_terms(queries, cumulated, gathered, block) + intra_part
    row_mean = jnp.mean(numerator, axis=-1, keepdims=True)
    centred = numerator - row_mean
    row_var = jnp.mean(centred * centred, axis=-1, keepdims=True)
    normed = (centred * lax.rsqrt(row_var + 1e-05) * norm_gain).astype(jnp.bfloat16)
    head_terms = jnp.einsum(
        "vtr,edrc->edvtc", normed, columns_all.reshape(inner_size, outer, head_size, -1),
        preferred_element_type=jnp.float32,
    ).astype(jnp.bfloat16)
    head_terms = jnp.roll(head_terms, lax.axis_index(SEQ[1]) - inner_size // 2, axis=0)
    head_terms = jnp.roll(head_terms, lax.axis_index(SEQ[0]) - outer // 2, axis=1)
    pair, across = HEAD
    pairs = lax.axis_size(pair)
    head_terms = head_terms.reshape(pairs, inner_size // pairs, *head_terms.shape[1:])
    blocks = jnp.transpose(head_terms, (0, 2, 1, 3, 4, 5))
    arrived = lax.all_to_all(blocks, pair, split_axis=0, concat_axis=0, tiled=True)
    pair_sum = jnp.sum(arrived.astype(jnp.float32), axis=0).astype(jnp.bfloat16)
    summed = lax.all_to_all(pair_sum, across, split_axis=0, concat_axis=0, tiled=True)
    summed = jnp.sum(summed.astype(jnp.float32), axis=0)
    summed = jnp.transpose(summed, (1, 2, 0, 3)).reshape(*normed.shape[:2], -1)
    return (residual_in[None, :, :].astype(jnp.float32) + summed).astype(jnp.bfloat16)


def solution(mesh):
    split = Mesh(
        mesh.devices.reshape(4, 8, mesh.shape["head"] // 2, 2, mesh.shape["var"]),
        ("seq_0", "seq_1", "head_0", "head_1", "var"),
    )
    heads = HEAD[::-1]
    placed = (
        P(SEQ, heads),
        P(SEQ, heads),
        P("var", SEQ),
        P(None, heads),
        P(heads, None, None),
        P(heads, None, None),
        P(heads, None),
        P(heads),
        P(heads, SEQ),
    )
    return jax.shard_map(
        body, mesh=split, in_specs=placed, out_specs=P("var", SEQ, heads), check_vma=False
    )
```
